128 devices in a mesh: dp: 8 (over x, core), sector: 16 (over y, z).
Axes of the slice: x: 4, y: 4, z: 4, core: 2. Of those that a mesh axis runs over, the one named last changes fastest.
Arguments:
- hits: bfloat16 [8, 32768, 256], P('dp', 'sector'), may hold values from -6 to 6
- tiles: bfloat16 [8, 256, 8, 128, 128], P('dp', 'sector'), may hold values from -0.1875 to 0.1875
- sources: int32 [8, 256, 8], P('dp', 'sector'), may hold values from 0 to 23
- send_list: int32 [8, 16, 2, 4], P('dp'), may hold values from 0 to 15, as said below
- w_message: bfloat16 [2, 256, 256], replicated, may hold values from -0.375 to 0.375
- w_self: bfloat16 [2, 256, 256], replicated, may hold values from -0.375 to 0.375
- cotangent: float32 [8, 32768, 256], P('dp', 'sector'), may hold values from -6 to 6
Outputs:
- hit_output: bfloat16 [8, 32768, 256], P('dp', 'sector')
- hit_grad: float32 [8, 32768, 256], P('dp', 'sector')
- message_grad: float32 [2, 256, 256], replicated
- self_grad: float32 [2, 256, 256], replicated
The draws below stay inside these ranges and needn't reach their ends.
Inputs may be any that keep to these rules, and one draw needn't show every extreme that they name: `send_list`: each list holds 4 distinct local block numbers of its sector.
All inputs are finite; a program needn't handle non-finite values.
Results may differ from the reference program's by a relative error of at most 0.007.
Values may be sent and summed in bfloat16 or wider, within the bound.
No kernel may reach another device: no remote copies, remote signals or barrier semaphores. Data moves between devices by JAX's collectives and lax.ppermute only.
A program may use at most 128 MiB of HBM per device.

```python
import jax
import jax.numpy as jnp
from jax import lax

F = 256
TILE = 128
K = 8
S = 4
LAYERS = 2
HB = 16
EVENTS = 8
SECTORS = 16
BLOCKS = 256
ROWS = 32768


def draw_send_list(key, part):
    scores = jax.random.randint(key, (EVENTS, SECTORS, 2, HB), 0, 1 << 20) * HB + jnp.arange(HB, dtype=jnp.int32)
    order = jnp.argsort(scores, axis=-1)
    return order[..., :S].astype(jnp.int32)


def set_ends(entries, rng, smallest, top_value):
    dims = entries.shape
    spot = [jax.random.randint(jax.random.fold_in(rng, axis), (), 0, dims[axis]) for axis in range(len(dims))]
    entries = entries.at[tuple(spot)].set(smallest)
    longest = dims.index(max(dims))
    spot[longest] = (spot[longest] + 1) % dims[longest]
    return entries.at[tuple(spot)].set(top_value)


def levels(own_key, dims, split, low, top_value):
    loudness = 1.0
    for position, shards_of in split:
        draws = jax.random.uniform(jax.random.fold_in(jax.random.fold_in(own_key, 6), position), (shards_of,), jnp.float32, low / len(split), top_value / len(split))
        loudness = loudness * jnp.repeat(jnp.exp(draws), dims[position] // shards_of).reshape((-1,) + (1,) * (len(dims) - 1 - position))
    return loudness


def gaussian(rng, extent, spread, most, split=(), kind=jnp.bfloat16):
    entries = spread * jax.random.normal(rng, extent, jnp.float32)
    if split:
        entries = entries * levels(rng, extent, split, -0.22, 0.18)
    return jnp.clip(entries, -most, most).astype(kind)


def setup_inputs(seed: int = 0) -> dict:
    keys = jax.random.split(jax.random.key(seed), 8)
    return {
        "hits": gaussian(keys[0], (EVENTS, ROWS, F), 1.0, 6.0, ((0, 8), (1, 16))),
        "tiles": gaussian(keys[1], (EVENTS, BLOCKS, K, TILE, TILE), (K * TILE) ** -0.5, 0.1875, ((0, 8), (1, 16))),
        "sources": set_ends(jax.random.randint(keys[2], (EVENTS, BLOCKS, K), 0, HB + 2 * S), jax.random.fold_in(keys[2], 1), 0, (HB + 2 * S) - 1).astype(jnp.int32),
        "send_list": draw_send_list(jax.random.fold_in(keys[7], 71), 0),
        "w_message": gaussian(keys[4], (LAYERS, F, F), F ** -0.5, 0.375),
        "w_self": gaussian(keys[5], (LAYERS, F, F), F ** -0.5, 0.375),
        "cotangent": gaussian(keys[6], (EVENTS, ROWS, F), 1.0, 6.0, ((0, 8), (1, 16)), jnp.float32),
    }


def silu_grad(pre):
    sig = jax.nn.sigmoid(pre)
    return sig * (1.0 + pre * (1.0 - sig))

def slot_table(message, send_list):
    blocks = message.reshape(SECTORS, HB, TILE, F)
    from_lower = jnp.take_along_axis(jnp.roll(blocks, 1, 0), jnp.roll(send_list, 1, 0)[:, 0, :, None, None], axis=1)
    from_upper = jnp.take_along_axis(jnp.roll(blocks, -1, 0), jnp.roll(send_list, -1, 0)[:, 1, :, None, None], axis=1)
    return jnp.concatenate([blocks, from_lower, from_upper], axis=1)

def sector_aggregate(args):
    table, sector_sources, sector_tiles = args
    gathered = table[sector_sources].astype(jnp.float32)
    return jnp.einsum('bkij,bkjf->bif', sector_tiles.astype(jnp.float32), gathered)

def sector_slot_grad(args):
    sector_sources, sector_tiles, sector_dpre = args
    contrib = jnp.einsum('bkij,bif->bkjf', sector_tiles.astype(jnp.float32), sector_dpre.astype(jnp.float32))
    empty = jnp.zeros((HB + 2 * S, TILE, F), jnp.float32)
    return empty.at[sector_sources.reshape(-1)].add(contrib.reshape(HB * K, TILE, F))

def add_lent(dblocks, lent_grad, indices):
    return dblocks.at[indices].add(lent_grad)

def one_event(hits, tiles, sources, send_list, w_message, w_self, cotangent):
    tiles_r = tiles.reshape(SECTORS, HB, K, TILE, TILE)
    sources_r = sources.reshape(SECTORS, HB, K)
    current = hits
    saved = []
    for layer_index in range(LAYERS):
        message = jnp.dot(current, w_message[layer_index], preferred_element_type=jnp.float32).astype(jnp.bfloat16)
        table = slot_table(message, send_list)
        aggregate = lax.map(sector_aggregate, (table, sources_r, tiles_r)).reshape(ROWS, F)
        pre = aggregate + jnp.dot(current, w_self[layer_index], preferred_element_type=jnp.float32)
        saved.append((current, pre))
        current = (current.astype(jnp.float32) + jax.nn.silu(pre)).astype(jnp.bfloat16)
    grad = cotangent
    message_steps = [None] * LAYERS
    self_steps = [None] * LAYERS
    for layer_index in reversed(range(LAYERS)):
        layer_in, pre = saved[layer_index]
        dpre = (grad * silu_grad(pre)).astype(jnp.bfloat16)
        slot_grad = lax.map(sector_slot_grad, (sources_r, tiles_r, dpre.reshape(SECTORS, HB, TILE, F)))
        dblocks = slot_grad[:, :HB]
        lower_slots = jnp.roll(slot_grad[:, HB:HB + S], -1, 0)
        upper_slots = jnp.roll(slot_grad[:, HB + S:], 1, 0)
        dblocks = jax.vmap(add_lent)(dblocks, lower_slots, send_list[:, 0])
        dblocks = jax.vmap(add_lent)(dblocks, upper_slots, send_list[:, 1])
        dmessage = dblocks.reshape(ROWS, F).astype(jnp.bfloat16)
        self_steps[layer_index] = jnp.dot(layer_in.T, dpre, preferred_element_type=jnp.float32)
        message_steps[layer_index] = jnp.dot(layer_in.T, dmessage, preferred_element_type=jnp.float32)
        grad = grad + jnp.dot(dpre, w_self[layer_index].T, preferred_element_type=jnp.float32)
        grad = grad + jnp.dot(dmessage, w_message[layer_index].T, preferred_element_type=jnp.float32)
    return (current, grad, jnp.stack(message_steps), jnp.stack(self_steps))

def reference(hits, tiles, sources, send_list, w_message, w_self, cotangent):

    def per_event(args):
        return one_event(args[0], args[1], args[2], args[3], w_message, w_self, args[4])
    outputs, grads, message_steps, self_steps = lax.map(per_event, (hits, tiles, sources, send_list, cotangent))
    scale = 1.0 / jnp.sqrt(jnp.float32(EVENTS * ROWS))
    return (outputs, grads, lax.optimization_barrier(jnp.sum(message_steps, axis=0)) * scale, lax.optimization_barrier(jnp.sum(self_steps, axis=0)) * scale)
```

```python
import jax
import jax.numpy as jnp
from jax import lax
from jax.sharding import PartitionSpec as P

LAYERS = 2


def extended_2(cells, sides, width):
    for axis, dim in sides:
        count = lax.axis_size(axis)
        head = lax.slice_in_dim(cells, 0, width, axis=dim)
        tail = lax.slice_in_dim(cells, cells.shape[dim] - width, cells.shape[dim], axis=dim)
        cells = jnp.concatenate(
            [
                lax.ppermute(tail, axis, [(i, (i + 1) % count) for i in range(count)]),
                cells,
                lax.ppermute(head, axis, [((i + 1) % count, i) for i in range(count)]),
            ],
            axis=dim,
        )
    return cells


def all_reduce(x, axes):
    count = lax.axis_size(axes)
    pieces = x.reshape(count, -1)
    mine = lax.all_to_all(pieces, axes, 0, 0, tiled=True).sum(0)
    spread = jnp.broadcast_to(mine[None], (count,) + mine.shape)
    return lax.all_to_all(spread, axes, 0, 0, tiled=True).reshape(x.shape)


def silu_grad(pre):
    sig = jax.nn.sigmoid(pre)
    return sig * (1.0 + pre * (1.0 - sig))


def per_device(hits, tiles, sources, send_list, w_message, w_self, cotangent):
    blocks_here = tiles.shape[1]
    tile_rows = tiles.shape[3]
    width = hits.shape[2]
    lent = send_list.shape[3]
    listed = tiles.shape[2]
    sector_here = lax.axis_index("sector")
    lists = send_list[0]
    own_lists = lax.dynamic_index_in_dim(lists, sector_here, 0, keepdims=False)
    tile_data = tiles[0]
    slot_ids = sources[0]
    slot_count = blocks_here + 2 * lent
    flat_ids = slot_ids.reshape(-1)
    current = hits[0]
    saved = []
    for layer_index in range(LAYERS):
        message = jnp.dot(
            current, w_message[layer_index], preferred_element_type=jnp.float32
        ).astype(jnp.bfloat16)
        message_blocks = message.reshape(blocks_here, tile_rows, width)
        packet = jnp.concatenate(
            [message_blocks[own_lists[1]], message_blocks[own_lists[0]]]
        ).reshape(2 * lent * tile_rows, width)
        extended = extended_2(packet, (("sector", 0),), lent * tile_rows)
        table = jnp.concatenate(
            [
                message_blocks,
                extended[: lent * tile_rows].reshape(lent, tile_rows, width),
                extended[-lent * tile_rows :].reshape(lent, tile_rows, width),
            ]
        )
        gathered = table[slot_ids]
        aggregate = jnp.einsum(
            "bkij,bkjf->bif", tile_data, gathered, preferred_element_type=jnp.float32
        )
        pre = aggregate.reshape(-1, width) + jnp.dot(
            current, w_self[layer_index], preferred_element_type=jnp.float32
        )
        saved.append((current, pre))
        current = (current.astype(jnp.float32) + jax.nn.silu(pre)).astype(jnp.bfloat16)
    grad = cotangent[0]
    message_steps = [None] * LAYERS
    self_steps = [None] * LAYERS
    for layer_index in reversed(range(LAYERS)):
        layer_in, pre = saved[layer_index]
        dpre = (grad * silu_grad(pre)).astype(jnp.bfloat16)
        contrib = jnp.einsum(
            "bkij,bif->bkjf",
            tile_data,
            dpre.reshape(blocks_here, tile_rows, width),
            preferred_element_type=jnp.float32,
        )
        slot_grad = jax.ops.segment_sum(
            contrib.reshape(blocks_here * listed, tile_rows * width),
            flat_ids,
            num_segments=slot_count,
        )
        packet = slot_grad[blocks_here:].reshape(2 * lent * tile_rows, width)
        extended = extended_2(packet, (("sector", 0),), lent * tile_rows)
        dblocks = slot_grad[:blocks_here].reshape(blocks_here, tile_rows, width)
        dblocks = dblocks.at[own_lists[1]].add(
            extended[: lent * tile_rows].reshape(lent, tile_rows, width)
        )
        dblocks = dblocks.at[own_lists[0]].add(
            extended[-lent * tile_rows :].reshape(lent, tile_rows, width)
        )
        dmessage = dblocks.reshape(-1, width).astype(jnp.bfloat16)
        self_part = jnp.dot(layer_in.T, dpre, preferred_element_type=jnp.float32)
        message_part = jnp.dot(layer_in.T, dmessage, preferred_element_type=jnp.float32)
        message_steps[layer_index] = message_part
        self_steps[layer_index] = self_part
        grad = grad + jnp.dot(dpre, w_self[layer_index].T, preferred_element_type=jnp.float32)
        grad = grad + jnp.dot(
            dmessage, w_message[layer_index].T, preferred_element_type=jnp.float32
        )
    message_total = jnp.stack(message_steps)
    self_total = jnp.stack(self_steps)
    both = all_reduce(jnp.stack([message_total, self_total]), ("dp", "sector"))
    message_total, self_total = both[0], both[1]
    total_rows = blocks_here * tile_rows * lax.axis_size(("dp", "sector"))
    scale = 1.0 / jnp.sqrt(jnp.float32(total_rows))
    return (current[None], grad[None], message_total * scale, self_total * scale)


def solution(mesh):
    in_specs = (
        P("dp", "sector", None),
        P("dp", "sector", None, None, None),
        P("dp", "sector", None),
        P("dp", None, None, None),
        P(),
        P(),
        P("dp", "sector", None),
    )
    out_specs = (P("dp", "sector", None), P("dp", "sector", None), P(), P())
    return jax.shard_map(
        per_device, mesh=mesh, in_specs=in_specs, out_specs=out_specs, check_vma=False
    )
```

```python
import jax
import jax.numpy as jnp
from jax import lax
from jax.experimental import pallas as pl
from jax.experimental.pallas import tpu as pltpu
from jax.sharding import PartitionSpec as P

LAYERS = 2
GROUP = 4


def aggregate_kernel(src_ref, tiles_ref, table_ref, out_ref):
    step = pl.program_id(0)
    for i in range(GROUP):
        block = step * GROUP + i
        acc = None
        for k in range(tiles_ref.shape[1]):
            slot = src_ref[block, k]
            part = jnp.dot(tiles_ref[i, k], table_ref[slot], preferred_element_type=jnp.float32)
            acc = part if acc is None else acc + part
        out_ref[i] = acc


def block_aggregate(slot_ids, tile_data, table):
    blocks, listed, rows, _ = tile_data.shape
    width = table.shape[-1]
    return pl.pallas_call(
        aggregate_kernel,
        grid_spec=pltpu.PrefetchScalarGridSpec(
            num_scalar_prefetch=1,
            grid=(blocks // GROUP,),
            in_specs=[
                pl.BlockSpec((GROUP, listed, rows, rows), lambda g, src: (g, 0, 0, 0)),
                pl.BlockSpec(table.shape, lambda g, src: (0, 0, 0)),
            ],
            out_specs=pl.BlockSpec((GROUP, rows, width), lambda g, src: (g, 0, 0)),
        ),
        out_shape=jax.ShapeDtypeStruct((blocks, rows, width), jnp.float32),
    )(slot_ids, tile_data, table)


def slot_grad_kernel(src_ref, tiles_ref, dpre_ref, out_ref):
    step = pl.program_id(0)

    @pl.when(step == 0)
    def _():
        out_ref[...] = jnp.zeros(out_ref.shape, out_ref.dtype)

    for i in range(GROUP):
        block = step * GROUP + i
        grad = dpre_ref[i]
        for k in range(tiles_ref.shape[1]):
            slot = src_ref[block, k]
            part = lax.dot_general(
                tiles_ref[i, k], grad, (((0,), (0,)), ((), ())),
                preferred_element_type=jnp.float32,
            )
            out_ref[slot] += part


def block_slot_grad(slot_ids, tile_data, dpre_blocks, slot_count):
    blocks, listed, rows, _ = tile_data.shape
    width = dpre_blocks.shape[-1]
    return pl.pallas_call(
        slot_grad_kernel,
        grid_spec=pltpu.PrefetchScalarGridSpec(
            num_scalar_prefetch=1,
            grid=(blocks // GROUP,),
            in_specs=[
                pl.BlockSpec((GROUP, listed, rows, rows), lambda g, src: (g, 0, 0, 0)),
                pl.BlockSpec((GROUP, rows, width), lambda g, src: (g, 0, 0)),
            ],
            out_specs=pl.BlockSpec((slot_count, rows, width), lambda g, src: (0, 0, 0)),
        ),
        out_shape=jax.ShapeDtypeStruct((slot_count, rows, width), jnp.float32),
        compiler_params=pltpu.CompilerParams(dimension_semantics=("arbitrary",)),
    )(slot_ids, tile_data, dpre_blocks)


def extended_2(cells, sides, width):
    for axis, dim in sides:
        count = lax.axis_size(axis)
        head = lax.slice_in_dim(cells, 0, width, axis=dim)
        tail = lax.slice_in_dim(cells, cells.shape[dim] - width, cells.shape[dim], axis=dim)
        cells = jnp.concatenate(
            [
                lax.ppermute(tail, axis, [(i, (i + 1) % count) for i in range(count)]),
                cells,
                lax.ppermute(head, axis, [((i + 1) % count, i) for i in range(count)]),
            ],
            axis=dim,
        )
    return cells


def all_reduce(x, axes):
    count = lax.axis_size(axes)
    pieces = x.reshape(count, -1)
    mine = lax.all_to_all(pieces, axes, 0, 0, tiled=True).sum(0)
    spread = jnp.broadcast_to(mine[None], (count,) + mine.shape)
    return lax.all_to_all(spread, axes, 0, 0, tiled=True).reshape(x.shape)


def silu_grad(pre):
    sig = jax.nn.sigmoid(pre)
    return sig * (1.0 + pre * (1.0 - sig))


def per_device(hits, tiles, sources, send_list, w_message, w_self, cotangent):
    blocks_here = tiles.shape[1]
    tile_rows = tiles.shape[3]
    width = hits.shape[2]
    lent = send_list.shape[3]
    listed = tiles.shape[2]
    sector_here = lax.axis_index("sector")
    lists = send_list[0]
    own_lists = lax.dynamic_index_in_dim(lists, sector_here, 0, keepdims=False)
    tile_data = tiles[0]
    slot_ids = sources[0]
    slot_count = blocks_here + 2 * lent
    current = hits[0]
    saved = []
    for layer_index in range(LAYERS):
        message = jnp.dot(
            current, w_message[layer_index], preferred_element_type=jnp.float32
        ).astype(jnp.bfloat16)
        message_blocks = message.reshape(blocks_here, tile_rows, width)
        packet = jnp.concatenate(
            [message_blocks[own_lists[1]], message_blocks[own_lists[0]]]
        ).reshape(2 * lent * tile_rows, width)
        extended = extended_2(packet, (("sector", 0),), lent * tile_rows)
        table = jnp.concatenate(
            [
                message_blocks,
                extended[: lent * tile_rows].reshape(lent, tile_rows, width),
                extended[-lent * tile_rows :].reshape(lent, tile_rows, width),
            ]
        )
        aggregate = block_aggregate(slot_ids, tile_data, table)
        pre = aggregate.reshape(-1, width) + jnp.dot(
            current, w_self[layer_index], preferred_element_type=jnp.float32
        )
        saved.append((current, pre))
        current = (current.astype(jnp.float32) + jax.nn.silu(pre)).astype(jnp.bfloat16)
    grad = cotangent[0]
    message_steps = [None] * LAYERS
    self_steps = [None] * LAYERS
    for layer_index in reversed(range(LAYERS)):
        layer_in, pre = saved[layer_index]
        dpre = (grad * silu_grad(pre)).astype(jnp.bfloat16)
        slot_grad = block_slot_grad(
            slot_ids, tile_data, dpre.reshape(blocks_here, tile_rows, width), slot_count
        )
        packet = slot_grad[blocks_here:].reshape(2 * lent * tile_rows, width)
        extended = extended_2(packet, (("sector", 0),), lent * tile_rows)
        dblocks = slot_grad[:blocks_here].reshape(blocks_here, tile_rows, width)
        dblocks = dblocks.at[own_lists[1]].add(
            extended[: lent * tile_rows].reshape(lent, tile_rows, width)
        )
        dblocks = dblocks.at[own_lists[0]].add(
            extended[-lent * tile_rows :].reshape(lent, tile_rows, width)
        )
        dmessage = dblocks.reshape(-1, width).astype(jnp.bfloat16)
        self_part = jnp.dot(layer_in.T, dpre, preferred_element_type=jnp.float32)
        message_part = jnp.dot(layer_in.T, dmessage, preferred_element_type=jnp.float32)
        message_steps[layer_index] = message_part
        self_steps[layer_index] = self_part
        grad = grad + jnp.dot(dpre, w_self[layer_index].T, preferred_element_type=jnp.float32)
        grad = grad + jnp.dot(
            dmessage, w_message[layer_index].T, preferred_element_type=jnp.float32
        )
    message_total = jnp.stack(message_steps)
    self_total = jnp.stack(self_steps)
    both = all_reduce(jnp.stack([message_total, self_total]), ("dp", "sector"))
    message_total, self_total = both[0], both[1]
    total_rows = blocks_here * tile_rows * lax.axis_size(("dp", "sector"))
    scale = 1.0 / jnp.sqrt(jnp.float32(total_rows))
    return (current[None], grad[None], message_total * scale, self_total * scale)


def solution(mesh):
    in_specs = (
        P("dp", "sector", None),
        P("dp", "sector", None, None, None),
        P("dp", "sector", None),
        P("dp", None, None, None),
        P(),
        P(),
        P("dp", "sector", None),
    )
    out_specs = (P("dp", "sector", None), P("dp", "sector", None), P(), P())
    return jax.shard_map(
        per_device, mesh=mesh, in_specs=in_specs, out_specs=out_specs, check_vma=False
    )
```

```python
import jax
import jax.numpy as jnp
from jax import lax
from jax.experimental import pallas as pl
from jax.experimental.pallas import tpu as pltpu
from jax.sharding import PartitionSpec as P

LAYERS = 2
GROUP = 8


def aggregate_kernel(src_ref, tiles_ref, table_ref, out_ref):
    step = pl.program_id(0)
    for i in range(GROUP):
        block = step * GROUP + i
        acc = None
        for k in range(tiles_ref.shape[1]):
            slot = src_ref[block, k]
            part = jnp.dot(tiles_ref[i, k], table_ref[slot], preferred_element_type=jnp.float32)
            acc = part if acc is None else acc + part
        out_ref[i] = acc


def block_aggregate(slot_ids, tile_data, table):
    blocks, listed, rows, _ = tile_data.shape
    width = table.shape[-1]
    return pl.pallas_call(
        aggregate_kernel,
        grid_spec=pltpu.PrefetchScalarGridSpec(
            num_scalar_prefetch=1,
            grid=(blocks // GROUP,),
            in_specs=[
                pl.BlockSpec((GROUP, listed, rows, rows), lambda g, src: (g, 0, 0, 0)),
                pl.BlockSpec(table.shape, lambda g, src: (0, 0, 0)),
            ],
            out_specs=pl.BlockSpec((GROUP, rows, width), lambda g, src: (g, 0, 0)),
        ),
        out_shape=jax.ShapeDtypeStruct((blocks, rows, width), jnp.float32),
    )(slot_ids, tile_data, table)


def slot_grad_kernel(src_ref, tiles_ref, dpre_ref, out_ref):
    step = pl.program_id(0)

    @pl.when(step == 0)
    def _():
        out_ref[...] = jnp.zeros(out_ref.shape, out_ref.dtype)

    for i in range(GROUP):
        block = step * GROUP + i
        grad = dpre_ref[i]
        for k in range(tiles_ref.shape[1]):
            slot = src_ref[block, k]
            part = lax.dot_general(
                tiles_ref[i, k], grad, (((0,), (0,)), ((), ())),
                preferred_element_type=jnp.float32,
            )
            out_ref[slot] += part


def block_slot_grad(slot_ids, tile_data, dpre_blocks, slot_count):
    blocks, listed, rows, _ = tile_data.shape
    width = dpre_blocks.shape[-1]
    return pl.pallas_call(
        slot_grad_kernel,
        grid_spec=pltpu.PrefetchScalarGridSpec(
            num_scalar_prefetch=1,
            grid=(blocks // GROUP,),
            in_specs=[
                pl.BlockSpec((GROUP, listed, rows, rows), lambda g, src: (g, 0, 0, 0)),
                pl.BlockSpec((GROUP, rows, width), lambda g, src: (g, 0, 0)),
            ],
            out_specs=pl.BlockSpec((slot_count, rows, width), lambda g, src: (0, 0, 0)),
        ),
        out_shape=jax.ShapeDtypeStruct((slot_count, rows, width), jnp.float32),
        compiler_params=pltpu.CompilerParams(dimension_semantics=("arbitrary",)),
    )(slot_ids, tile_data, dpre_blocks)


def fold_kernel(lists_ref, slot_ref, lower_ref, upper_ref, out_ref, acc_ref):
    acc_ref[...] = slot_ref[...]
    for i in range(lower_ref.shape[0]):
        block = lists_ref[1, i]
        acc_ref[block] += lower_ref[i]
    for i in range(upper_ref.shape[0]):
        block = lists_ref[0, i]
        acc_ref[block] += upper_ref[i]
    out_ref[...] = acc_ref[...].astype(out_ref.dtype)


def fold_lent(own_lists, slot_grad, from_lower, from_upper, blocks):
    _, rows, width = slot_grad.shape
    lent = from_lower.shape[0]
    return pl.pallas_call(
        fold_kernel,
        grid_spec=pltpu.PrefetchScalarGridSpec(
            num_scalar_prefetch=1,
            grid=(1,),
            in_specs=[
                pl.BlockSpec((blocks, rows, width), lambda g, lists: (0, 0, 0)),
                pl.BlockSpec((lent, rows, width), lambda g, lists: (0, 0, 0)),
                pl.BlockSpec((lent, rows, width), lambda g, lists: (0, 0, 0)),
            ],
            out_specs=pl.BlockSpec((blocks, rows, width), lambda g, lists: (0, 0, 0)),
            scratch_shapes=[pltpu.VMEM((blocks, rows, width), jnp.float32)],
        ),
        out_shape=jax.ShapeDtypeStruct((blocks, rows, width), jnp.bfloat16),
    )(own_lists, slot_grad, from_lower, from_upper)


def to_upper(x, axis):
    count = lax.axis_size(axis)
    return lax.ppermute(x, axis, [(i, (i + 1) % count) for i in range(count)])


def to_lower(x, axis):
    count = lax.axis_size(axis)
    return lax.ppermute(x, axis, [((i + 1) % count, i) for i in range(count)])


def all_reduce(x, axes):
    count = lax.axis_size(axes)
    pieces = x.reshape(count, -1)
    mine = lax.all_to_all(pieces, axes, 0, 0, tiled=True).sum(0)
    spread = jnp.broadcast_to(mine[None], (count,) + mine.shape)
    return lax.all_to_all(spread, axes, 0, 0, tiled=True).reshape(x.shape)


def silu_grad(pre):
    sig = jax.nn.sigmoid(pre)
    return sig * (1.0 + pre * (1.0 - sig))


def per_device(hits, tiles, sources, send_list, w_message, w_self, cotangent):
    blocks_here = tiles.shape[1]
    tile_rows = tiles.shape[3]
    width = hits.shape[2]
    lent = send_list.shape[3]
    listed = tiles.shape[2]
    sector_here = lax.axis_index("sector")
    lists = send_list[0]
    own_lists = lax.dynamic_index_in_dim(lists, sector_here, 0, keepdims=False)
    tile_data = tiles[0]
    slot_ids = sources[0]
    slot_count = blocks_here + 2 * lent
    current = hits[0]
    saved = []
    for layer_index in range(LAYERS):
        message = jnp.dot(
            current, w_message[layer_index], preferred_element_type=jnp.float32
        ).astype(jnp.bfloat16)
        message_blocks = message.reshape(blocks_here, tile_rows, width)
        from_lower = to_upper(message_blocks[own_lists[0]], "sector")
        from_upper = to_lower(message_blocks[own_lists[1]], "sector")
        table = jnp.concatenate([message_blocks, from_lower, from_upper])
        aggregate = block_aggregate(slot_ids, tile_data, table)
        pre = aggregate.reshape(-1, width) + jnp.dot(
            current, w_self[layer_index], preferred_element_type=jnp.float32
        )
        saved.append((current, pre))
        current = (current.astype(jnp.float32) + jax.nn.silu(pre)).astype(jnp.bfloat16)
    grad = cotangent[0]
    message_steps = [None] * LAYERS
    self_steps = [None] * LAYERS
    for layer_index in reversed(range(LAYERS)):
        layer_in, pre = saved[layer_index]
        dpre = (grad * silu_grad(pre)).astype(jnp.bfloat16)
        slot_grad = block_slot_grad(
            slot_ids, tile_data, dpre.reshape(blocks_here, tile_rows, width), slot_count
        )
        lent_down_grad = to_upper(slot_grad[blocks_here + lent :], "sector")
        lent_up_grad = to_lower(slot_grad[blocks_here : blocks_here + lent], "sector")
        dmessage = fold_lent(
            own_lists, slot_grad, lent_down_grad, lent_up_grad, blocks_here
        ).reshape(-1, width)
        self_part = jnp.dot(layer_in.T, dpre, preferred_element_type=jnp.float32)
        message_part = jnp.dot(layer_in.T, dmessage, preferred_element_type=jnp.float32)
        message_steps[layer_index] = message_part
        self_steps[layer_index] = self_part
        grad = grad + jnp.dot(dpre, w_self[layer_index].T, preferred_element_type=jnp.float32)
        grad = grad + jnp.dot(
            dmessage, w_message[layer_index].T, preferred_element_type=jnp.float32
        )
    message_total = jnp.stack(message_steps)
    self_total = jnp.stack(self_steps)
    both = all_reduce(jnp.stack([message_total, self_total]), ("dp", "sector"))
    message_total, self_total = both[0], both[1]
    total_rows = blocks_here * tile_rows * lax.axis_size(("dp", "sector"))
    scale = 1.0 / jnp.sqrt(jnp.float32(total_rows))
    return (current[None], grad[None], message_total * scale, self_total * scale)


def solution(mesh):
    in_specs = (
        P("dp", "sector", None),
        P("dp", "sector", None, None, None),
        P("dp", "sector", None),
        P("dp", None, None, None),
        P(),
        P(),
        P("dp", "sector", None),
    )
    out_specs = (P("dp", "sector", None), P("dp", "sector", None), P(), P())
    return jax.shard_map(
        per_device, mesh=mesh, in_specs=in_specs, out_specs=out_specs, check_vma=False
    )
```

```python
import functools

import jax
import jax.numpy as jnp
from jax import lax
from jax.experimental import pallas as pl
from jax.experimental.pallas import tpu as pltpu
from jax.sharding import PartitionSpec as P

LAYERS = 2
GROUP = 8


def aggregate_kernel(lo, src_ref, tiles_ref, table_ref, *rest):
    out_ref = rest[-1]
    count = table_ref.shape[0]
    step = pl.program_id(0)

    def one_block(i, carry):
        block = step * GROUP + i
        if len(rest) == 2:
            out_ref[i] = rest[0][i]
        else:
            out_ref[i] = jnp.zeros(out_ref.shape[1:], out_ref.dtype)
        for k in range(tiles_ref.shape[1]):
            slot = src_ref[block, k] - lo

            @pl.when((slot >= 0) & (slot < count))
            def _():
                out_ref[i] += jnp.dot(
                    tiles_ref[i, k], table_ref[slot], preferred_element_type=jnp.float32
                )

        return carry

    lax.fori_loop(0, GROUP, one_block, 0)


def block_aggregate(slot_ids, tile_data, table, lo, start=None):
    blocks, listed, rows, _ = tile_data.shape
    width = table.shape[-1]
    in_specs = [
        pl.BlockSpec((GROUP, listed, rows, rows), lambda g, src: (g, 0, 0, 0)),
        pl.BlockSpec(table.shape, lambda g, src: (0, 0, 0)),
    ]
    args = [slot_ids, tile_data, table]
    aliases = {}
    if start is not None:
        in_specs.append(pl.BlockSpec((GROUP, rows, width), lambda g, src: (g, 0, 0)))
        args.append(start)
        aliases = {3: 0}
    return pl.pallas_call(
        functools.partial(aggregate_kernel, lo),
        grid_spec=pltpu.PrefetchScalarGridSpec(
            num_scalar_prefetch=1,
            grid=(blocks // GROUP,),
            in_specs=in_specs,
            out_specs=pl.BlockSpec((GROUP, rows, width), lambda g, src: (g, 0, 0)),
        ),
        out_shape=jax.ShapeDtypeStruct((blocks, rows, width), jnp.float32),
        input_output_aliases=aliases,
    )(*args)


def slot_grad_kernel(lo, src_ref, tiles_ref, dpre_ref, out_ref):
    count = out_ref.shape[0]
    step = pl.program_id(0)

    @pl.when(step == 0)
    def _():
        out_ref[...] = jnp.zeros(out_ref.shape, out_ref.dtype)

    def one_block(i, carry):
        block = step * GROUP + i
        for k in range(tiles_ref.shape[1]):
            slot = src_ref[block, k] - lo

            @pl.when((slot >= 0) & (slot < count))
            def _():
                out_ref[slot] += lax.dot_general(
                    tiles_ref[i, k], dpre_ref[i], (((0,), (0,)), ((), ())),
                    preferred_element_type=jnp.float32,
                )

        return carry

    lax.fori_loop(0, GROUP, one_block, 0)


def block_slot_grad(slot_ids, tile_data, dpre_blocks, lo, count):
    blocks, listed, rows, _ = tile_data.shape
    width = dpre_blocks.shape[-1]
    return pl.pallas_call(
        functools.partial(slot_grad_kernel, lo),
        grid_spec=pltpu.PrefetchScalarGridSpec(
            num_scalar_prefetch=1,
            grid=(blocks // GROUP,),
            in_specs=[
                pl.BlockSpec((GROUP, listed, rows, rows), lambda g, src: (g, 0, 0, 0)),
                pl.BlockSpec((GROUP, rows, width), lambda g, src: (g, 0, 0)),
            ],
            out_specs=pl.BlockSpec((count, rows, width), lambda g, src: (0, 0, 0)),
        ),
        out_shape=jax.ShapeDtypeStruct((count, rows, width), jnp.float32),
        compiler_params=pltpu.CompilerParams(dimension_semantics=("arbitrary",)),
    )(slot_ids, tile_data, dpre_blocks)


def fold_kernel(lists_ref, slot_ref, lower_ref, upper_ref, out_ref, acc_ref):
    acc_ref[...] = slot_ref[...]
    for i in range(lower_ref.shape[0]):
        block = lists_ref[1, i]
        acc_ref[block] += lower_ref[i]
    for i in range(upper_ref.shape[0]):
        block = lists_ref[0, i]
        acc_ref[block] += upper_ref[i]
    out_ref[...] = acc_ref[...].astype(out_ref.dtype)


def fold_lent(own_lists, slot_grad, from_lower, from_upper, blocks):
    _, rows, width = slot_grad.shape
    lent = from_lower.shape[0]
    return pl.pallas_call(
        fold_kernel,
        grid_spec=pltpu.PrefetchScalarGridSpec(
            num_scalar_prefetch=1,
            grid=(1,),
            in_specs=[
                pl.BlockSpec((blocks, rows, width), lambda g, lists: (0, 0, 0)),
                pl.BlockSpec((lent, rows, width), lambda g, lists: (0, 0, 0)),
                pl.BlockSpec((lent, rows, width), lambda g, lists: (0, 0, 0)),
            ],
            out_specs=pl.BlockSpec((blocks, rows, width), lambda g, lists: (0, 0, 0)),
            scratch_shapes=[pltpu.VMEM((blocks, rows, width), jnp.float32)],
        ),
        out_shape=jax.ShapeDtypeStruct((blocks, rows, width), jnp.bfloat16),
    )(own_lists, slot_grad, from_lower, from_upper)


def to_upper(x, axis):
    count = lax.axis_size(axis)
    return lax.ppermute(x, axis, [(i, (i + 1) % count) for i in range(count)])


def to_lower(x, axis):
    count = lax.axis_size(axis)
    return lax.ppermute(x, axis, [((i + 1) % count, i) for i in range(count)])


def all_reduce(x, axes):
    count = lax.axis_size(axes)
    pieces = x.reshape(count, -1)
    mine = lax.all_to_all(pieces, axes, 0, 0, tiled=True).sum(0)
    spread = jnp.broadcast_to(mine[None], (count,) + mine.shape)
    return lax.all_to_all(spread, axes, 0, 0, tiled=True).reshape(x.shape)


def silu_grad(pre):
    sig = jax.nn.sigmoid(pre)
    return sig * (1.0 + pre * (1.0 - sig))


def per_device(hits, tiles, sources, send_list, w_message, w_self, cotangent):
    blocks_here = tiles.shape[1]
    tile_rows = tiles.shape[3]
    width = hits.shape[2]
    lent = send_list.shape[3]
    listed = tiles.shape[2]
    sector_here = lax.axis_index("sector")
    lists = send_list[0]
    own_lists = lax.dynamic_index_in_dim(lists, sector_here, 0, keepdims=False)
    tile_data = tiles[0]
    slot_ids = sources[0]
    slot_count = blocks_here + 2 * lent
    current = hits[0]
    saved = []
    for layer_index in range(LAYERS):
        message = jnp.dot(
            current, w_message[layer_index], preferred_element_type=jnp.float32
        ).astype(jnp.bfloat16)
        message_blocks = message.reshape(blocks_here, tile_rows, width)
        from_lower = to_upper(message_blocks[own_lists[0]], "sector")
        from_upper = to_lower(message_blocks[own_lists[1]], "sector")
        own_part = block_aggregate(slot_ids, tile_data, message_blocks, 0)
        lent_table = jnp.concatenate([from_lower, from_upper])
        aggregate = block_aggregate(slot_ids, tile_data, lent_table, blocks_here, own_part)
        pre = aggregate.reshape(-1, width) + jnp.dot(
            current, w_self[layer_index], preferred_element_type=jnp.float32
        )
        saved.append((current, pre))
        current = (current.astype(jnp.float32) + jax.nn.silu(pre)).astype(jnp.bfloat16)
    grad = cotangent[0]
    message_steps = [None] * LAYERS
    self_steps = [None] * LAYERS
    for layer_index in reversed(range(LAYERS)):
        layer_in, pre = saved[layer_index]
        dpre = (grad * silu_grad(pre)).astype(jnp.bfloat16)
        dpre_blocks = dpre.reshape(blocks_here, tile_rows, width)
        lent_grad = block_slot_grad(slot_ids, tile_data, dpre_blocks, blocks_here, 2 * lent)
        lent_down_grad = to_upper(lent_grad[lent:], "sector")
        lent_up_grad = to_lower(lent_grad[:lent], "sector")
        own_grad = block_slot_grad(slot_ids, tile_data, dpre_blocks, 0, blocks_here)
        dmessage = fold_lent(
            own_lists, own_grad, lent_down_grad, lent_up_grad, blocks_here
        ).reshape(-1, width)
        self_part = jnp.dot(layer_in.T, dpre, preferred_element_type=jnp.float32)
        message_part = jnp.dot(layer_in.T, dmessage, preferred_element_type=jnp.float32)
        message_steps[layer_index] = message_part
        self_steps[layer_index] = self_part
        grad = grad + jnp.dot(dpre, w_self[layer_index].T, preferred_element_type=jnp.float32)
        grad = grad + jnp.dot(
            dmessage, w_message[layer_index].T, preferred_element_type=jnp.float32
        )
    message_total = jnp.stack(message_steps)
    self_total = jnp.stack(self_steps)
    both = all_reduce(jnp.stack([message_total, self_total]), ("dp", "sector"))
    message_total, self_total = both[0], both[1]
    total_rows = blocks_here * tile_rows * lax.axis_size(("dp", "sector"))
    scale = 1.0 / jnp.sqrt(jnp.float32(total_rows))
    return (current[None], grad[None], message_total * scale, self_total * scale)


def solution(mesh):
    in_specs = (
        P("dp", "sector", None),
        P("dp", "sector", None, None, None),
        P("dp", "sector", None),
        P("dp", None, None, None),
        P(),
        P(),
        P("dp", "sector", None),
    )
    out_specs = (P("dp", "sector", None), P("dp", "sector", None), P(), P())
    return jax.shard_map(
        per_device, mesh=mesh, in_specs=in_specs, out_specs=out_specs, check_vma=False
    )
```

```python
import jax
import jax.numpy as jnp
from jax import lax
from jax.experimental import pallas as pl
from jax.experimental.pallas import tpu as pltpu
from jax.sharding import PartitionSpec as P

LAYERS = 2
GROUP = 8


def aggregate_kernel(src_ref, tiles_ref, table_ref, out_ref):
    step = pl.program_id(0)
    for i in range(GROUP):
        block = step * GROUP + i
        acc = None
        for k in range(tiles_ref.shape[1]):
            slot = src_ref[block, k]
            part = jnp.dot(tiles_ref[i, k], table_ref[slot], preferred_element_type=jnp.float32)
            acc = part if acc is None else acc + part
        out_ref[i] = acc


def block_aggregate(slot_ids, tile_data, table):
    blocks, listed, rows, _ = tile_data.shape
    width = table.shape[-1]
    return pl.pallas_call(
        aggregate_kernel,
        grid_spec=pltpu.PrefetchScalarGridSpec(
            num_scalar_prefetch=1,
            grid=(blocks // GROUP,),
            in_specs=[
                pl.BlockSpec((GROUP, listed, rows, rows), lambda g, src: (g, 0, 0, 0)),
                pl.BlockSpec(table.shape, lambda g, src: (0, 0, 0)),
            ],
            out_specs=pl.BlockSpec((GROUP, rows, width), lambda g, src: (g, 0, 0)),
        ),
        out_shape=jax.ShapeDtypeStruct((blocks, rows, width), jnp.float32),
    )(slot_ids, tile_data, table)


def slot_grad_kernel(src_ref, tiles_ref, dpre_ref, out_ref):
    step = pl.program_id(0)

    @pl.when(step == 0)
    def _():
        out_ref[...] = jnp.zeros(out_ref.shape, out_ref.dtype)

    for i in range(GROUP):
        block = step * GROUP + i
        grad = dpre_ref[i]
        for k in range(tiles_ref.shape[1]):
            slot = src_ref[block, k]
            part = lax.dot_general(
                tiles_ref[i, k], grad, (((0,), (0,)), ((), ())),
                preferred_element_type=jnp.float32,
            )
            out_ref[slot] += part


def block_slot_grad(slot_ids, tile_data, dpre_blocks, slot_count):
    blocks, listed, rows, _ = tile_data.shape
    width = dpre_blocks.shape[-1]
    return pl.pallas_call(
        slot_grad_kernel,
        grid_spec=pltpu.PrefetchScalarGridSpec(
            num_scalar_prefetch=1,
            grid=(blocks // GROUP,),
            in_specs=[
                pl.BlockSpec((GROUP, listed, rows, rows), lambda g, src: (g, 0, 0, 0)),
                pl.BlockSpec((GROUP, rows, width), lambda g, src: (g, 0, 0)),
            ],
            out_specs=pl.BlockSpec((slot_count, rows, width), lambda g, src: (0, 0, 0)),
        ),
        out_shape=jax.ShapeDtypeStruct((slot_count, rows, width), jnp.float32),
        compiler_params=pltpu.CompilerParams(dimension_semantics=("arbitrary",)),
    )(slot_ids, tile_data, dpre_blocks)


def fold_kernel(lists_ref, slot_ref, lower_ref, upper_ref, out_ref, acc_ref):
    acc_ref[...] = slot_ref[...]
    for i in range(lower_ref.shape[0]):
        block = lists_ref[1, i]
        acc_ref[block] += lower_ref[i]
    for i in range(upper_ref.shape[0]):
        block = lists_ref[0, i]
        acc_ref[block] += upper_ref[i]
    out_ref[...] = acc_ref[...].astype(out_ref.dtype)


def fold_lent(own_lists, slot_grad, from_lower, from_upper, blocks):
    _, rows, width = slot_grad.shape
    lent = from_lower.shape[0]
    return pl.pallas_call(
        fold_kernel,
        grid_spec=pltpu.PrefetchScalarGridSpec(
            num_scalar_prefetch=1,
            grid=(1,),
            in_specs=[
                pl.BlockSpec((blocks, rows, width), lambda g, lists: (0, 0, 0)),
                pl.BlockSpec((lent, rows, width), lambda g, lists: (0, 0, 0)),
                pl.BlockSpec((lent, rows, width), lambda g, lists: (0, 0, 0)),
            ],
            out_specs=pl.BlockSpec((blocks, rows, width), lambda g, lists: (0, 0, 0)),
            scratch_shapes=[pltpu.VMEM((blocks, rows, width), jnp.float32)],
        ),
        out_shape=jax.ShapeDtypeStruct((blocks, rows, width), jnp.bfloat16),
    )(own_lists, slot_grad, from_lower, from_upper)


def to_upper(x, axis):
    count = lax.axis_size(axis)
    return lax.ppermute(x, axis, [(i, (i + 1) % count) for i in range(count)])


def to_lower(x, axis):
    count = lax.axis_size(axis)
    return lax.ppermute(x, axis, [((i + 1) % count, i) for i in range(count)])


def all_reduce(x, axes):
    count = lax.axis_size(axes)
    pieces = x.reshape(count, -1)
    mine = lax.all_to_all(pieces, axes, 0, 0, tiled=True).sum(0)
    spread = jnp.broadcast_to(mine[None], (count,) + mine.shape)
    return lax.all_to_all(spread, axes, 0, 0, tiled=True).reshape(x.shape)


def silu_grad(pre):
    sig = jax.nn.sigmoid(pre)
    return sig * (1.0 + pre * (1.0 - sig))


def per_device(hits, tiles, sources, send_list, w_message, w_self, cotangent):
    blocks_here = tiles.shape[1]
    tile_rows = tiles.shape[3]
    width = hits.shape[2]
    lent = send_list.shape[3]
    listed = tiles.shape[2]
    sector_here = lax.axis_index("sector")
    lists = send_list[0]
    own_lists = lax.dynamic_index_in_dim(lists, sector_here, 0, keepdims=False)
    tile_data = tiles[0]
    slot_ids = sources[0]
    slot_count = blocks_here + 2 * lent
    current = hits[0]
    saved = []
    for layer_index in range(LAYERS):
        message = jnp.dot(
            current, w_message[layer_index], preferred_element_type=jnp.float32
        ).astype(jnp.bfloat16)
        message_blocks = message.reshape(blocks_here, tile_rows, width)
        current_blocks = current.reshape(blocks_here, tile_rows, width)
        lent_rows = jnp.concatenate(
            [
                to_upper(current_blocks[own_lists[0]], "sector"),
                to_lower(current_blocks[own_lists[1]], "sector"),
            ]
        )
        lent_message = jnp.dot(
            lent_rows.reshape(-1, width), w_message[layer_index],
            preferred_element_type=jnp.float32,
        ).astype(jnp.bfloat16)
        table = jnp.concatenate(
            [message_blocks, lent_message.reshape(2 * lent, tile_rows, width)]
        )
        aggregate = block_aggregate(slot_ids, tile_data, table)
        pre = aggregate.reshape(-1, width) + jnp.dot(
            current, w_self[layer_index], preferred_element_type=jnp.float32
        )
        saved.append((current, lent_rows, pre))
        current = (current.astype(jnp.float32) + jax.nn.silu(pre)).astype(jnp.bfloat16)
    grad = cotangent[0]
    message_steps = [None] * LAYERS
    self_steps = [None] * LAYERS
    for layer_index in reversed(range(LAYERS)):
        layer_in, lent_rows, pre = saved[layer_index]
        dpre = (grad * silu_grad(pre)).astype(jnp.bfloat16)
        slot_grad = block_slot_grad(
            slot_ids, tile_data, dpre.reshape(blocks_here, tile_rows, width), slot_count
        )
        lent_down_grad = to_upper(slot_grad[blocks_here + lent :], "sector")
        lent_up_grad = to_lower(slot_grad[blocks_here : blocks_here + lent], "sector")
        dmessage = fold_lent(
            own_lists, slot_grad, lent_down_grad, lent_up_grad, blocks_here
        ).reshape(-1, width)
        self_part = jnp.dot(layer_in.T, dpre, preferred_element_type=jnp.float32)
        slot_rows = jnp.concatenate(
            [layer_in.reshape(blocks_here, tile_rows, width), lent_rows]
        ).reshape(-1, width)
        flat_grad = slot_grad.reshape(-1, width)
        grad_high = flat_grad.astype(jnp.bfloat16)
        grad_low = (flat_grad - grad_high.astype(jnp.float32)).astype(jnp.bfloat16)
        message_part = jnp.dot(
            slot_rows.T, grad_high, preferred_element_type=jnp.float32
        ) + jnp.dot(slot_rows.T, grad_low, preferred_element_type=jnp.float32)
        message_steps[layer_index] = message_part
        self_steps[layer_index] = self_part
        grad = grad + jnp.dot(dpre, w_self[layer_index].T, preferred_element_type=jnp.float32)
        grad = grad + jnp.dot(
            dmessage, w_message[layer_index].T, preferred_element_type=jnp.float32
        )
    message_total = jnp.stack(message_steps)
    self_total = jnp.stack(self_steps)
    both = all_reduce(jnp.stack([message_total, self_total]), ("dp", "sector"))
    message_total, self_total = both[0], both[1]
    total_rows = blocks_here * tile_rows * lax.axis_size(("dp", "sector"))
    scale = 1.0 / jnp.sqrt(jnp.float32(total_rows))
    return (current[None], grad[None], message_total * scale, self_total * scale)


def solution(mesh):
    in_specs = (
        P("dp", "sector", None),
        P("dp", "sector", None, None, None),
        P("dp", "sector", None),
        P("dp", None, None, None),
        P(),
        P(),
        P("dp", "sector", None),
    )
    out_specs = (P("dp", "sector", None), P("dp", "sector", None), P(), P())
    return jax.shard_map(
        per_device, mesh=mesh, in_specs=in_specs, out_specs=out_specs, check_vma=False
    )
```

```python
import jax
import jax.numpy as jnp
from jax import lax
from jax.experimental import pallas as pl
from jax.experimental.pallas import tpu as pltpu
from jax.sharding import PartitionSpec as P

LAYERS = 2
GROUP = 8


def layer_kernel(src_ref, tiles_ref, table_ref, hits_ref, weight_ref, pre_ref, out_ref):
    step = pl.program_id(0)
    listed = tiles_ref.shape[1]
    for i in range(GROUP):
        block = step * GROUP + i
        lhs = jnp.concatenate([tiles_ref[i, k] for k in range(listed)], axis=1)
        rhs = jnp.concatenate(
            [table_ref[src_ref[block, k]] for k in range(listed)], axis=0
        )
        rows = hits_ref[i]
        pre = jnp.dot(lhs, rhs, preferred_element_type=jnp.float32) + jnp.dot(
            rows, weight_ref[...], preferred_element_type=jnp.float32
        )
        pre_ref[i] = pre
        out_ref[i] = (rows.astype(jnp.float32) + pre * jax.nn.sigmoid(pre)).astype(
            out_ref.dtype
        )


def block_layer(slot_ids, tile_data, table, hit_blocks, weight):
    blocks, listed, rows, _ = tile_data.shape
    width = table.shape[-1]
    block_spec = pl.BlockSpec((GROUP, rows, width), lambda g, src: (g, 0, 0))
    return pl.pallas_call(
        layer_kernel,
        grid_spec=pltpu.PrefetchScalarGridSpec(
            num_scalar_prefetch=1,
            grid=(blocks // GROUP,),
            in_specs=[
                pl.BlockSpec((GROUP, listed, rows, rows), lambda g, src: (g, 0, 0, 0)),
                pl.BlockSpec(table.shape, lambda g, src: (0, 0, 0)),
                block_spec,
                pl.BlockSpec(weight.shape, lambda g, src: (0, 0)),
            ],
            out_specs=[block_spec, block_spec],
        ),
        out_shape=[
            jax.ShapeDtypeStruct((blocks, rows, width), jnp.float32),
            jax.ShapeDtypeStruct((blocks, rows, width), hit_blocks.dtype),
        ],
    )(slot_ids, tile_data, table, hit_blocks, weight)


def slot_grad_kernel(src_ref, tiles_ref, dpre_ref, out_ref):
    step = pl.program_id(0)

    @pl.when(step == 0)
    def _():
        out_ref[...] = jnp.zeros(out_ref.shape, out_ref.dtype)

    for i in range(GROUP):
        block = step * GROUP + i
        grad = dpre_ref[i]
        for k in range(tiles_ref.shape[1]):
            slot = src_ref[block, k]
            part = lax.dot_general(
                tiles_ref[i, k], grad, (((0,), (0,)), ((), ())),
                preferred_element_type=jnp.float32,
            )
            out_ref[slot] += part


def block_slot_grad(slot_ids, tile_data, dpre_blocks, slot_count):
    blocks, listed, rows, _ = tile_data.shape
    width = dpre_blocks.shape[-1]
    return pl.pallas_call(
        slot_grad_kernel,
        grid_spec=pltpu.PrefetchScalarGridSpec(
            num_scalar_prefetch=1,
            grid=(blocks // GROUP,),
            in_specs=[
                pl.BlockSpec((GROUP, listed, rows, rows), lambda g, src: (g, 0, 0, 0)),
                pl.BlockSpec((GROUP, rows, width), lambda g, src: (g, 0, 0)),
            ],
            out_specs=pl.BlockSpec((slot_count, rows, width), lambda g, src: (0, 0, 0)),
        ),
        out_shape=jax.ShapeDtypeStruct((slot_count, rows, width), jnp.float32),
        compiler_params=pltpu.CompilerParams(dimension_semantics=("arbitrary",)),
    )(slot_ids, tile_data, dpre_blocks)


def fold_kernel(lists_ref, slot_ref, lower_ref, upper_ref, out_ref, acc_ref):
    acc_ref[...] = slot_ref[...]
    for i in range(lower_ref.shape[0]):
        block = lists_ref[1, i]
        acc_ref[block] += lower_ref[i]
    for i in range(upper_ref.shape[0]):
        block = lists_ref[0, i]
        acc_ref[block] += upper_ref[i]
    out_ref[...] = acc_ref[...].astype(out_ref.dtype)


def fold_lent(own_lists, slot_grad, from_lower, from_upper, blocks):
    _, rows, width = slot_grad.shape
    lent = from_lower.shape[0]
    return pl.pallas_call(
        fold_kernel,
        grid_spec=pltpu.PrefetchScalarGridSpec(
            num_scalar_prefetch=1,
            grid=(1,),
            in_specs=[
                pl.BlockSpec((blocks, rows, width), lambda g, lists: (0, 0, 0)),
                pl.BlockSpec((lent, rows, width), lambda g, lists: (0, 0, 0)),
                pl.BlockSpec((lent, rows, width), lambda g, lists: (0, 0, 0)),
            ],
            out_specs=pl.BlockSpec((blocks, rows, width), lambda g, lists: (0, 0, 0)),
            scratch_shapes=[pltpu.VMEM((blocks, rows, width), jnp.float32)],
        ),
        out_shape=jax.ShapeDtypeStruct((blocks, rows, width), jnp.bfloat16),
    )(own_lists, slot_grad, from_lower, from_upper)


def to_upper(x, axis):
    count = lax.axis_size(axis)
    return lax.ppermute(x, axis, [(i, (i + 1) % count) for i in range(count)])


def to_lower(x, axis):
    count = lax.axis_size(axis)
    return lax.ppermute(x, axis, [((i + 1) % count, i) for i in range(count)])


def all_reduce(x, axes):
    count = lax.axis_size(axes)
    pieces = x.reshape(count, -1)
    mine = lax.all_to_all(pieces, axes, 0, 0, tiled=True).sum(0)
    spread = jnp.broadcast_to(mine[None], (count,) + mine.shape)
    return lax.all_to_all(spread, axes, 0, 0, tiled=True).reshape(x.shape)


def silu_grad(pre):
    sig = jax.nn.sigmoid(pre)
    return sig * (1.0 + pre * (1.0 - sig))


def per_device(hits, tiles, sources, send_list, w_message, w_self, cotangent):
    blocks_here = tiles.shape[1]
    tile_rows = tiles.shape[3]
    width = hits.shape[2]
    lent = send_list.shape[3]
    listed = tiles.shape[2]
    sector_here = lax.axis_index("sector")
    lists = send_list[0]
    own_lists = lax.dynamic_index_in_dim(lists, sector_here, 0, keepdims=False)
    tile_data = tiles[0]
    slot_ids = sources[0]
    slot_count = blocks_here + 2 * lent
    current = hits[0]
    saved = []
    for layer_index in range(LAYERS):
        message = jnp.dot(
            current, w_message[layer_index], preferred_element_type=jnp.float32
        ).astype(jnp.bfloat16)
        message_blocks = message.reshape(blocks_here, tile_rows, width)
        from_lower = to_upper(message_blocks[own_lists[0]], "sector")
        from_upper = to_lower(message_blocks[own_lists[1]], "sector")
        table = jnp.concatenate([message_blocks, from_lower, from_upper])
        pre, following = block_layer(
            slot_ids, tile_data, table, current.reshape(message_blocks.shape),
            w_self[layer_index],
        )
        saved.append((current, pre.reshape(-1, width)))
        current = following.reshape(-1, width)
    grad = cotangent[0]
    message_steps = [None] * LAYERS
    self_steps = [None] * LAYERS
    for layer_index in reversed(range(LAYERS)):
        layer_in, pre = saved[layer_index]
        dpre = (grad * silu_grad(pre)).astype(jnp.bfloat16)
        slot_grad = block_slot_grad(
            slot_ids, tile_data, dpre.reshape(blocks_here, tile_rows, width), slot_count
        )
        lent_down_grad = to_upper(slot_grad[blocks_here + lent :], "sector")
        lent_up_grad = to_lower(slot_grad[blocks_here : blocks_here + lent], "sector")
        dmessage = fold_lent(
            own_lists, slot_grad, lent_down_grad, lent_up_grad, blocks_here
        ).reshape(-1, width)
        self_part = jnp.dot(layer_in.T, dpre, preferred_element_type=jnp.float32)
        message_part = jnp.dot(layer_in.T, dmessage, preferred_element_type=jnp.float32)
        message_steps[layer_index] = message_part
        self_steps[layer_index] = self_part
        grad = grad + jnp.dot(dpre, w_self[layer_index].T, preferred_element_type=jnp.float32)
        grad = grad + jnp.dot(
            dmessage, w_message[layer_index].T, preferred_element_type=jnp.float32
        )
    message_total = jnp.stack(message_steps)
    self_total = jnp.stack(self_steps)
    both = all_reduce(jnp.stack([message_total, self_total]), ("dp", "sector"))
    message_total, self_total = both[0], both[1]
    total_rows = blocks_here * tile_rows * lax.axis_size(("dp", "sector"))
    scale = 1.0 / jnp.sqrt(jnp.float32(total_rows))
    return (current[None], grad[None], message_total * scale, self_total * scale)


def solution(mesh):
    in_specs = (
        P("dp", "sector", None),
        P("dp", "sector", None, None, None),
        P("dp", "sector", None),
        P("dp", None, None, None),
        P(),
        P(),
        P("dp", "sector", None),
    )
    out_specs = (P("dp", "sector", None), P("dp", "sector", None), P(), P())
    return jax.shard_map(
        per_device, mesh=mesh, in_specs=in_specs, out_specs=out_specs, check_vma=False
    )
```

```python
import jax
import jax.numpy as jnp
from jax import lax
from jax.experimental import pallas as pl
from jax.experimental.pallas import tpu as pltpu
from jax.sharding import PartitionSpec as P

LAYERS = 2
GROUP = 8


def layer_kernel(src_ref, tiles_ref, table_ref, hits_ref, weight_ref, pre_ref, out_ref):
    step = pl.program_id(0)
    listed = tiles_ref.shape[1]
    for i in range(GROUP):
        block = step * GROUP + i
        lhs = jnp.concatenate([tiles_ref[i, k] for k in range(listed)], axis=1)
        rhs = jnp.concatenate(
            [table_ref[src_ref[block, k]] for k in range(listed)], axis=0
        )
        rows = hits_ref[i]
        pre = jnp.dot(lhs, rhs, preferred_element_type=jnp.float32) + jnp.dot(
            rows, weight_ref[...], preferred_element_type=jnp.float32
        )
        pre_ref[i] = pre
        out_ref[i] = (rows.astype(jnp.float32) + pre * jax.nn.sigmoid(pre)).astype(
            out_ref.dtype
        )


def block_layer(slot_ids, tile_data, table, hit_blocks, weight):
    blocks, listed, rows, _ = tile_data.shape
    width = table.shape[-1]
    block_spec = pl.BlockSpec((GROUP, rows, width), lambda g, src: (g, 0, 0))
    return pl.pallas_call(
        layer_kernel,
        grid_spec=pltpu.PrefetchScalarGridSpec(
            num_scalar_prefetch=1,
            grid=(blocks // GROUP,),
            in_specs=[
                pl.BlockSpec((GROUP, listed, rows, rows), lambda g, src: (g, 0, 0, 0)),
                pl.BlockSpec(table.shape, lambda g, src: (0, 0, 0)),
                block_spec,
                pl.BlockSpec(weight.shape, lambda g, src: (0, 0)),
            ],
            out_specs=[block_spec, block_spec],
        ),
        out_shape=[
            jax.ShapeDtypeStruct((blocks, rows, width), jnp.float32),
            jax.ShapeDtypeStruct((blocks, rows, width), hit_blocks.dtype),
        ],
    )(slot_ids, tile_data, table, hit_blocks, weight)


def slot_grad_kernel(src_ref, tiles_ref, dpre_ref, out_ref):
    step = pl.program_id(0)

    @pl.when(step == 0)
    def _():
        out_ref[...] = jnp.zeros(out_ref.shape, out_ref.dtype)

    for i in range(GROUP):
        block = step * GROUP + i
        grad = dpre_ref[i]
        for k in range(tiles_ref.shape[1]):
            slot = src_ref[block, k]
            part = lax.dot_general(
                tiles_ref[i, k], grad, (((0,), (0,)), ((), ())),
                preferred_element_type=jnp.float32,
            )
            out_ref[slot] += part


def block_slot_grad(slot_ids, tile_data, dpre_blocks, slot_count):
    blocks, listed, rows, _ = tile_data.shape
    width = dpre_blocks.shape[-1]
    return pl.pallas_call(
        slot_grad_kernel,
        grid_spec=pltpu.PrefetchScalarGridSpec(
            num_scalar_prefetch=1,
            grid=(blocks // GROUP,),
            in_specs=[
                pl.BlockSpec((GROUP, listed, rows, rows), lambda g, src: (g, 0, 0, 0)),
                pl.BlockSpec((GROUP, rows, width), lambda g, src: (g, 0, 0)),
            ],
            out_specs=pl.BlockSpec((slot_count, rows, width), lambda g, src: (0, 0, 0)),
        ),
        out_shape=jax.ShapeDtypeStruct((slot_count, rows, width), jnp.float32),
        compiler_params=pltpu.CompilerParams(dimension_semantics=("arbitrary",)),
    )(slot_ids, tile_data, dpre_blocks)


def fold_kernel(lists_ref, slot_ref, lower_ref, upper_ref, out_ref, acc_ref):
    acc_ref[...] = slot_ref[...]
    for i in range(lower_ref.shape[0]):
        block = lists_ref[1, i]
        acc_ref[block] += lower_ref[i]
    for i in range(upper_ref.shape[0]):
        block = lists_ref[0, i]
        acc_ref[block] += upper_ref[i]
    out_ref[...] = acc_ref[...].astype(out_ref.dtype)


def fold_lent(own_lists, slot_grad, from_lower, from_upper, blocks):
    _, rows, width = slot_grad.shape
    lent = from_lower.shape[0]
    return pl.pallas_call(
        fold_kernel,
        grid_spec=pltpu.PrefetchScalarGridSpec(
            num_scalar_prefetch=1,
            grid=(1,),
            in_specs=[
                pl.BlockSpec((blocks, rows, width), lambda g, lists: (0, 0, 0)),
                pl.BlockSpec((lent, rows, width), lambda g, lists: (0, 0, 0)),
                pl.BlockSpec((lent, rows, width), lambda g, lists: (0, 0, 0)),
            ],
            out_specs=pl.BlockSpec((blocks, rows, width), lambda g, lists: (0, 0, 0)),
            scratch_shapes=[pltpu.VMEM((blocks, rows, width), jnp.float32)],
        ),
        out_shape=jax.ShapeDtypeStruct((blocks, rows, width), jnp.bfloat16),
    )(own_lists, slot_grad, from_lower, from_upper)


def to_upper(x, axis):
    count = lax.axis_size(axis)
    return lax.ppermute(x, axis, [(i, (i + 1) % count) for i in range(count)])


def to_lower(x, axis):
    count = lax.axis_size(axis)
    return lax.ppermute(x, axis, [((i + 1) % count, i) for i in range(count)])


def all_reduce(x, axes, scale):
    count = lax.axis_size(axes)
    width = x.shape[-1]
    pieces = x.reshape(count, -1, width)
    mine = lax.all_to_all(pieces, axes, 0, 0, tiled=True).sum(0) * scale
    spread = jnp.broadcast_to(mine[None], (count,) + mine.shape)
    return lax.all_to_all(spread, axes, 0, 0, tiled=True).reshape(x.shape)


def silu_grad(pre):
    sig = jax.nn.sigmoid(pre)
    return sig * (1.0 + pre * (1.0 - sig))


def per_device(hits, tiles, sources, send_list, w_message, w_self, cotangent):
    blocks_here = tiles.shape[1]
    tile_rows = tiles.shape[3]
    width = hits.shape[2]
    lent = send_list.shape[3]
    listed = tiles.shape[2]
    sector_here = lax.axis_index("sector")
    lists = send_list[0]
    own_lists = lax.dynamic_index_in_dim(lists, sector_here, 0, keepdims=False)
    tile_data = tiles[0]
    slot_ids = sources[0]
    slot_count = blocks_here + 2 * lent
    current = hits[0]
    saved = []
    for layer_index in range(LAYERS):
        message = jnp.dot(
            current, w_message[layer_index], preferred_element_type=jnp.float32
        ).astype(jnp.bfloat16)
        message_blocks = message.reshape(blocks_here, tile_rows, width)
        from_lower = to_upper(message_blocks[own_lists[0]], "sector")
        from_upper = to_lower(message_blocks[own_lists[1]], "sector")
        table = jnp.concatenate([message_blocks, from_lower, from_upper])
        pre, following = block_layer(
            slot_ids, tile_data, table, current.reshape(message_blocks.shape),
            w_self[layer_index],
        )
        saved.append((current, pre.reshape(-1, width)))
        current = following.reshape(-1, width)
    grad = cotangent[0]
    message_steps = [None] * LAYERS
    self_steps = [None] * LAYERS
    for layer_index in reversed(range(LAYERS)):
        layer_in, pre = saved[layer_index]
        dpre = (grad * silu_grad(pre)).astype(jnp.bfloat16)
        slot_grad = block_slot_grad(
            slot_ids, tile_data, dpre.reshape(blocks_here, tile_rows, width), slot_count
        )
        lent_down_grad = to_upper(slot_grad[blocks_here + lent :], "sector")
        lent_up_grad = to_lower(slot_grad[blocks_here : blocks_here + lent], "sector")
        dmessage = fold_lent(
            own_lists, slot_grad, lent_down_grad, lent_up_grad, blocks_here
        ).reshape(-1, width)
        self_part = jnp.dot(layer_in.T, dpre, preferred_element_type=jnp.float32)
        message_part = jnp.dot(layer_in.T, dmessage, preferred_element_type=jnp.float32)
        message_steps[layer_index] = message_part
        self_steps[layer_index] = self_part
        grad = grad + jnp.dot(dpre, w_self[layer_index].T, preferred_element_type=jnp.float32)
        grad = grad + jnp.dot(
            dmessage, w_message[layer_index].T, preferred_element_type=jnp.float32
        )
    message_total = jnp.stack(message_steps)
    self_total = jnp.stack(self_steps)
    total_rows = blocks_here * tile_rows * lax.axis_size(("dp", "sector"))
    scale = 1.0 / jnp.sqrt(jnp.float32(total_rows))
    both = all_reduce(jnp.stack([message_total, self_total]), ("dp", "sector"), scale)
    return (current[None], grad[None], both[0], both[1])


def solution(mesh):
    in_specs = (
        P("dp", "sector", None),
        P("dp", "sector", None, None, None),
        P("dp", "sector", None),
        P("dp", None, None, None),
        P(),
        P(),
        P("dp", "sector", None),
    )
    out_specs = (P("dp", "sector", None), P("dp", "sector", None), P(), P())
    return jax.shard_map(
        per_device, mesh=mesh, in_specs=in_specs, out_specs=out_specs, check_vma=False
    )
```

```python
import jax
import jax.numpy as jnp
from jax import lax
from jax.experimental import pallas as pl
from jax.experimental.pallas import tpu as pltpu
from jax.sharding import PartitionSpec as P

LAYERS = 2
GROUP = 8


def slot_rows(own_ref, lent_ref, slot):
    own = own_ref.shape[0]
    return jnp.where(
        slot < own,
        own_ref[jnp.minimum(slot, own - 1)],
        lent_ref[jnp.maximum(slot - own, 0)],
    )


def layer_kernel(src_ref, tiles_ref, own_ref, lent_ref, hits_ref, weight_ref, pre_ref, out_ref):
    step = pl.program_id(0)
    listed = tiles_ref.shape[1]
    for i in range(GROUP):
        block = step * GROUP + i
        lhs = jnp.concatenate([tiles_ref[i, k] for k in range(listed)], axis=1)
        rhs = jnp.concatenate(
            [slot_rows(own_ref, lent_ref, src_ref[block, k]) for k in range(listed)], axis=0
        )
        rows = hits_ref[i]
        pre = jnp.dot(lhs, rhs, preferred_element_type=jnp.float32) + jnp.dot(
            rows, weight_ref[...], preferred_element_type=jnp.float32
        )
        pre_ref[i] = pre
        out_ref[i] = (rows.astype(jnp.float32) + pre * jax.nn.sigmoid(pre)).astype(
            out_ref.dtype
        )


def block_layer(slot_ids, tile_data, own_table, lent_table, hit_blocks, weight):
    blocks, listed, rows, _ = tile_data.shape
    width = own_table.shape[-1]
    block_spec = pl.BlockSpec((GROUP, rows, width), lambda g, src: (g, 0, 0))
    return pl.pallas_call(
        layer_kernel,
        grid_spec=pltpu.PrefetchScalarGridSpec(
            num_scalar_prefetch=1,
            grid=(blocks // GROUP,),
            in_specs=[
                pl.BlockSpec((GROUP, listed, rows, rows), lambda g, src: (g, 0, 0, 0)),
                pl.BlockSpec(own_table.shape, lambda g, src: (0, 0, 0)),
                pl.BlockSpec(lent_table.shape, lambda g, src: (0, 0, 0)),
                block_spec,
                pl.BlockSpec(weight.shape, lambda g, src: (0, 0)),
            ],
            out_specs=[block_spec, block_spec],
        ),
        out_shape=[
            jax.ShapeDtypeStruct((blocks, rows, width), jnp.float32),
            jax.ShapeDtypeStruct((blocks, rows, width), hit_blocks.dtype),
        ],
    )(slot_ids, tile_data, own_table, lent_table, hit_blocks, weight)


def slot_grad_kernel(src_ref, tiles_ref, dpre_ref, own_ref, lent_ref, out_ref):
    step = pl.program_id(0)

    @pl.when(step == 0)
    def _():
        out_ref[...] = jnp.zeros(out_ref.shape, out_ref.dtype)

    for i in range(GROUP):
        block = step * GROUP + i
        grad = dpre_ref[i]
        for k in range(tiles_ref.shape[1]):
            slot = src_ref[block, k]
            part = lax.dot_general(
                tiles_ref[i, k], grad, (((0,), (0,)), ((), ())),
                preferred_element_type=jnp.float32,
            )
            out_ref[slot] += part

    @pl.when(step == pl.num_programs(0) - 1)
    def _():
        own = own_ref.shape[0]
        own_ref[...] = out_ref[:own]
        lent_ref[...] = out_ref[own:]


def block_slot_grad(slot_ids, tile_data, dpre_blocks, slot_count):
    blocks, listed, rows, _ = tile_data.shape
    width = dpre_blocks.shape[-1]
    return pl.pallas_call(
        slot_grad_kernel,
        grid_spec=pltpu.PrefetchScalarGridSpec(
            num_scalar_prefetch=1,
            grid=(blocks // GROUP,),
            in_specs=[
                pl.BlockSpec((GROUP, listed, rows, rows), lambda g, src: (g, 0, 0, 0)),
                pl.BlockSpec((GROUP, rows, width), lambda g, src: (g, 0, 0)),
            ],
            out_specs=[
                pl.BlockSpec((blocks, rows, width), lambda g, src: (0, 0, 0)),
                pl.BlockSpec((slot_count - blocks, rows, width), lambda g, src: (0, 0, 0)),
            ],
            scratch_shapes=[pltpu.VMEM((slot_count, rows, width), jnp.float32)],
        ),
        out_shape=[
            jax.ShapeDtypeStruct((blocks, rows, width), jnp.float32),
            jax.ShapeDtypeStruct((slot_count - blocks, rows, width), jnp.float32),
        ],
        compiler_params=pltpu.CompilerParams(dimension_semantics=("arbitrary",)),
    )(slot_ids, tile_data, dpre_blocks)


def fold_kernel(lists_ref, slot_ref, lower_ref, upper_ref, out_ref, acc_ref):
    acc_ref[...] = slot_ref[...]
    for i in range(lower_ref.shape[0]):
        block = lists_ref[1, i]
        acc_ref[block] += lower_ref[i]
    for i in range(upper_ref.shape[0]):
        block = lists_ref[0, i]
        acc_ref[block] += upper_ref[i]
    out_ref[...] = acc_ref[...].astype(out_ref.dtype)


def fold_lent(own_lists, slot_grad, from_lower, from_upper, blocks):
    _, rows, width = slot_grad.shape
    lent = from_lower.shape[0]
    return pl.pallas_call(
        fold_kernel,
        grid_spec=pltpu.PrefetchScalarGridSpec(
            num_scalar_prefetch=1,
            grid=(1,),
            in_specs=[
                pl.BlockSpec((blocks, rows, width), lambda g, lists: (0, 0, 0)),
                pl.BlockSpec((lent, rows, width), lambda g, lists: (0, 0, 0)),
                pl.BlockSpec((lent, rows, width), lambda g, lists: (0, 0, 0)),
            ],
            out_specs=pl.BlockSpec((blocks, rows, width), lambda g, lists: (0, 0, 0)),
            scratch_shapes=[pltpu.VMEM((blocks, rows, width), jnp.float32)],
        ),
        out_shape=jax.ShapeDtypeStruct((blocks, rows, width), jnp.bfloat16),
    )(own_lists, slot_grad, from_lower, from_upper)


def to_upper(x, axis):
    count = lax.axis_size(axis)
    return lax.ppermute(x, axis, [(i, (i + 1) % count) for i in range(count)])


def to_lower(x, axis):
    count = lax.axis_size(axis)
    return lax.ppermute(x, axis, [((i + 1) % count, i) for i in range(count)])


def all_reduce(x, axes, scale):
    count = lax.axis_size(axes)
    width = x.shape[-1]
    pieces = x.reshape(count, -1, width)
    mine = lax.all_to_all(pieces, axes, 0, 0, tiled=True).sum(0) * scale
    spread = jnp.broadcast_to(mine[None], (count,) + mine.shape)
    return lax.all_to_all(spread, axes, 0, 0, tiled=True).reshape(x.shape)


def silu_grad(pre):
    sig = jax.nn.sigmoid(pre)
    return sig * (1.0 + pre * (1.0 - sig))


def per_device(hits, tiles, sources, send_list, w_message, w_self, cotangent):
    blocks_here = tiles.shape[1]
    tile_rows = tiles.shape[3]
    width = hits.shape[2]
    lent = send_list.shape[3]
    listed = tiles.shape[2]
    sector_here = lax.axis_index("sector")
    lists = send_list[0]
    own_lists = lax.dynamic_index_in_dim(lists, sector_here, 0, keepdims=False)
    tile_data = tiles[0]
    slot_ids = sources[0]
    slot_count = blocks_here + 2 * lent
    current = hits[0]
    saved = []
    for layer_index in range(LAYERS):
        message = jnp.dot(
            current, w_message[layer_index], preferred_element_type=jnp.float32
        ).astype(jnp.bfloat16)
        message_blocks = message.reshape(blocks_here, tile_rows, width)
        from_lower = to_upper(message_blocks[own_lists[0]], "sector")
        from_upper = to_lower(message_blocks[own_lists[1]], "sector")
        pre, following = block_layer(
            slot_ids, tile_data, message_blocks, jnp.concatenate([from_lower, from_upper]),
            current.reshape(message_blocks.shape),
            w_self[layer_index],
        )
        saved.append((current, pre.reshape(-1, width)))
        current = following.reshape(-1, width)
    grad = cotangent[0]
    message_steps = [None] * LAYERS
    self_steps = [None] * LAYERS
    for layer_index in reversed(range(LAYERS)):
        layer_in, pre = saved[layer_index]
        dpre = (grad * silu_grad(pre)).astype(jnp.bfloat16)
        own_grad, lent_grad = block_slot_grad(
            slot_ids, tile_data, dpre.reshape(blocks_here, tile_rows, width), slot_count
        )
        lent_down_grad = to_upper(lent_grad[lent:], "sector")
        lent_up_grad = to_lower(lent_grad[:lent], "sector")
        dmessage = fold_lent(
            own_lists, own_grad, lent_down_grad, lent_up_grad, blocks_here
        ).reshape(-1, width)
        self_part = jnp.dot(layer_in.T, dpre, preferred_element_type=jnp.float32)
        message_part = jnp.dot(layer_in.T, dmessage, preferred_element_type=jnp.float32)
        message_steps[layer_index] = message_part
        self_steps[layer_index] = self_part
        grad = grad + jnp.dot(dpre, w_self[layer_index].T, preferred_element_type=jnp.float32)
        grad = grad + jnp.dot(
            dmessage, w_message[layer_index].T, preferred_element_type=jnp.float32
        )
    message_total = jnp.stack(message_steps)
    self_total = jnp.stack(self_steps)
    total_rows = blocks_here * tile_rows * lax.axis_size(("dp", "sector"))
    scale = 1.0 / jnp.sqrt(jnp.float32(total_rows))
    both = all_reduce(jnp.stack([message_total, self_total]), ("dp", "sector"), scale)
    return (current[None], grad[None], both[0], both[1])


def solution(mesh):
    in_specs = (
        P("dp", "sector", None),
        P("dp", "sector", None, None, None),
        P("dp", "sector", None),
        P("dp", None, None, None),
        P(),
        P(),
        P("dp", "sector", None),
    )
    out_specs = (P("dp", "sector", None), P("dp", "sector", None), P(), P())
    return jax.shard_map(
        per_device, mesh=mesh, in_specs=in_specs, out_specs=out_specs, check_vma=False
    )
```

```python
import jax
import jax.numpy as jnp
from jax import lax
from jax.experimental import pallas as pl
from jax.experimental.pallas import tpu as pltpu
from jax.sharding import PartitionSpec as P

LAYERS = 2
GROUP = 8


def slot_rows(own_ref, lent_ref, slot):
    own = own_ref.shape[0]
    return jnp.where(
        slot < own,
        own_ref[jnp.minimum(slot, own - 1)],
        lent_ref[jnp.maximum(slot - own, 0)],
    )


def layer_kernel(src_ref, tiles_ref, own_ref, lent_ref, hits_ref, weight_ref, pre_ref, out_ref):
    step = pl.program_id(0)
    listed = tiles_ref.shape[1]
    for i in range(GROUP):
        block = step * GROUP + i
        lhs = jnp.concatenate([tiles_ref[i, k] for k in range(listed)], axis=1)
        rhs = jnp.concatenate(
            [slot_rows(own_ref, lent_ref, src_ref[block, k]) for k in range(listed)], axis=0
        )
        rows = hits_ref[i]
        pre = jnp.dot(lhs, rhs, preferred_element_type=jnp.float32) + jnp.dot(
            rows, weight_ref[...], preferred_element_type=jnp.float32
        )
        pre_ref[i] = pre
        out_ref[i] = (rows.astype(jnp.float32) + pre * jax.nn.sigmoid(pre)).astype(
            out_ref.dtype
        )


def block_layer(slot_ids, tile_data, own_table, lent_table, hit_blocks, weight):
    blocks, listed, rows, _ = tile_data.shape
    width = own_table.shape[-1]
    block_spec = pl.BlockSpec((GROUP, rows, width), lambda g, src: (g, 0, 0))
    return pl.pallas_call(
        layer_kernel,
        grid_spec=pltpu.PrefetchScalarGridSpec(
            num_scalar_prefetch=1,
            grid=(blocks // GROUP,),
            in_specs=[
                pl.BlockSpec((GROUP, listed, rows, rows), lambda g, src: (g, 0, 0, 0)),
                pl.BlockSpec(own_table.shape, lambda g, src: (0, 0, 0)),
                pl.BlockSpec(lent_table.shape, lambda g, src: (0, 0, 0)),
                block_spec,
                pl.BlockSpec(weight.shape, lambda g, src: (0, 0)),
            ],
            out_specs=[block_spec, block_spec],
        ),
        out_shape=[
            jax.ShapeDtypeStruct((blocks, rows, width), jnp.float32),
            jax.ShapeDtypeStruct((blocks, rows, width), hit_blocks.dtype),
        ],
    )(slot_ids, tile_data, own_table, lent_table, hit_blocks, weight)


def slot_grad_kernel(src_ref, tiles_ref, grad_ref, pre_ref, own_ref, low_ref, high_ref, dpre_ref, out_ref):
    step = pl.program_id(0)

    @pl.when(step == 0)
    def _():
        out_ref[...] = jnp.zeros(out_ref.shape, out_ref.dtype)

    for i in range(GROUP):
        block = step * GROUP + i
        pre = pre_ref[i]
        sig = jax.nn.sigmoid(pre)
        grad = (grad_ref[i] * (sig * (1.0 + pre * (1.0 - sig)))).astype(dpre_ref.dtype)
        dpre_ref[i] = grad
        for k in range(tiles_ref.shape[1]):
            slot = src_ref[block, k]
            part = lax.dot_general(
                tiles_ref[i, k], grad, (((0,), (0,)), ((), ())),
                preferred_element_type=jnp.float32,
            )
            out_ref[slot] += part

    @pl.when(step == pl.num_programs(0) - 1)
    def _():
        own = own_ref.shape[0]
        lent = low_ref.shape[0]
        own_ref[...] = out_ref[:own]
        low_ref[...] = out_ref[own : own + lent]
        high_ref[...] = out_ref[own + lent :]


def block_slot_grad(slot_ids, tile_data, grad_blocks, pre_blocks, slot_count):
    blocks, listed, rows, _ = tile_data.shape
    width = grad_blocks.shape[-1]
    lent = (slot_count - blocks) // 2
    block_spec = pl.BlockSpec((GROUP, rows, width), lambda g, src: (g, 0, 0))
    whole = lambda count: pl.BlockSpec((count, rows, width), lambda g, src: (0, 0, 0))
    return pl.pallas_call(
        slot_grad_kernel,
        grid_spec=pltpu.PrefetchScalarGridSpec(
            num_scalar_prefetch=1,
            grid=(blocks // GROUP,),
            in_specs=[
                pl.BlockSpec((GROUP, listed, rows, rows), lambda g, src: (g, 0, 0, 0)),
                block_spec,
                block_spec,
            ],
            out_specs=[whole(blocks), whole(lent), whole(lent), block_spec],
            scratch_shapes=[pltpu.VMEM((slot_count, rows, width), jnp.float32)],
        ),
        out_shape=[
            jax.ShapeDtypeStruct((blocks, rows, width), jnp.float32),
            jax.ShapeDtypeStruct((lent, rows, width), jnp.float32),
            jax.ShapeDtypeStruct((lent, rows, width), jnp.float32),
            jax.ShapeDtypeStruct((blocks, rows, width), jnp.bfloat16),
        ],
        compiler_params=pltpu.CompilerParams(dimension_semantics=("arbitrary",)),
    )(slot_ids, tile_data, grad_blocks, pre_blocks)


def fold_kernel(lists_ref, slot_ref, lower_ref, upper_ref, out_ref, acc_ref):
    acc_ref[...] = slot_ref[...]
    for i in range(lower_ref.shape[0]):
        block = lists_ref[1, i]
        acc_ref[block] += lower_ref[i]
    for i in range(upper_ref.shape[0]):
        block = lists_ref[0, i]
        acc_ref[block] += upper_ref[i]
    out_ref[...] = acc_ref[...].astype(out_ref.dtype)


def fold_lent(own_lists, slot_grad, from_lower, from_upper, blocks):
    _, rows, width = slot_grad.shape
    lent = from_lower.shape[0]
    return pl.pallas_call(
        fold_kernel,
        grid_spec=pltpu.PrefetchScalarGridSpec(
            num_scalar_prefetch=1,
            grid=(1,),
            in_specs=[
                pl.BlockSpec((blocks, rows, width), lambda g, lists: (0, 0, 0)),
                pl.BlockSpec((lent, rows, width), lambda g, lists: (0, 0, 0)),
                pl.BlockSpec((lent, rows, width), lambda g, lists: (0, 0, 0)),
            ],
            out_specs=pl.BlockSpec((blocks, rows, width), lambda g, lists: (0, 0, 0)),
            scratch_shapes=[pltpu.VMEM((blocks, rows, width), jnp.float32)],
        ),
        out_shape=jax.ShapeDtypeStruct((blocks, rows, width), jnp.bfloat16),
    )(own_lists, slot_grad, from_lower, from_upper)


def to_upper(x, axis):
    count = lax.axis_size(axis)
    return lax.ppermute(x, axis, [(i, (i + 1) % count) for i in range(count)])


def to_lower(x, axis):
    count = lax.axis_size(axis)
    return lax.ppermute(x, axis, [((i + 1) % count, i) for i in range(count)])


def all_reduce(x, axes, scale):
    count = lax.axis_size(axes)
    width = x.shape[-1]
    pieces = x.reshape(count, -1, width)
    mine = lax.all_to_all(pieces, axes, 0, 0, tiled=True).sum(0) * scale
    spread = jnp.broadcast_to(mine[None], (count,) + mine.shape)
    return lax.all_to_all(spread, axes, 0, 0, tiled=True).reshape(x.shape)


def silu_grad(pre):
    sig = jax.nn.sigmoid(pre)
    return sig * (1.0 + pre * (1.0 - sig))


def per_device(hits, tiles, sources, send_list, w_message, w_self, cotangent):
    blocks_here = tiles.shape[1]
    tile_rows = tiles.shape[3]
    width = hits.shape[2]
    lent = send_list.shape[3]
    listed = tiles.shape[2]
    sector_here = lax.axis_index("sector")
    lists = send_list[0]
    own_lists = lax.dynamic_index_in_dim(lists, sector_here, 0, keepdims=False)
    tile_data = tiles[0]
    slot_ids = sources[0]
    slot_count = blocks_here + 2 * lent
    current = hits[0]
    saved = []
    for layer_index in range(LAYERS):
        message = jnp.dot(
            current, w_message[layer_index], preferred_element_type=jnp.float32
        ).astype(jnp.bfloat16)
        message_blocks = message.reshape(blocks_here, tile_rows, width)
        from_lower = to_upper(message_blocks[own_lists[0]], "sector")
        from_upper = to_lower(message_blocks[own_lists[1]], "sector")
        pre, following = block_layer(
            slot_ids, tile_data, message_blocks, jnp.concatenate([from_lower, from_upper]),
            current.reshape(message_blocks.shape),
            w_self[layer_index],
        )
        saved.append((current, pre.reshape(-1, width)))
        current = following.reshape(-1, width)
    grad = cotangent[0]
    message_steps = [None] * LAYERS
    self_steps = [None] * LAYERS
    for layer_index in reversed(range(LAYERS)):
        layer_in, pre = saved[layer_index]
        own_grad, low_grad, high_grad, dpre_blocks = block_slot_grad(
            slot_ids, tile_data, grad.reshape(blocks_here, tile_rows, width),
            pre.reshape(blocks_here, tile_rows, width), slot_count,
        )
        dpre = dpre_blocks.reshape(-1, width)
        lent_down_grad = to_upper(high_grad, "sector")
        lent_up_grad = to_lower(low_grad, "sector")
        dmessage = fold_lent(
            own_lists, own_grad, lent_down_grad, lent_up_grad, blocks_here
        ).reshape(-1, width)
        self_part = jnp.dot(layer_in.T, dpre, preferred_element_type=jnp.float32)
        message_part = jnp.dot(layer_in.T, dmessage, preferred_element_type=jnp.float32)
        message_steps[layer_index] = message_part
        self_steps[layer_index] = self_part
        grad = grad + jnp.dot(dpre, w_self[layer_index].T, preferred_element_type=jnp.float32)
        grad = grad + jnp.dot(
            dmessage, w_message[layer_index].T, preferred_element_type=jnp.float32
        )
    message_total = jnp.stack(message_steps)
    self_total = jnp.stack(self_steps)
    total_rows = blocks_here * tile_rows * lax.axis_size(("dp", "sector"))
    scale = 1.0 / jnp.sqrt(jnp.float32(total_rows))
    both = all_reduce(jnp.stack([message_total, self_total]), ("dp", "sector"), scale)
    return (current[None], grad[None], both[0], both[1])


def solution(mesh):
    in_specs = (
        P("dp", "sector", None),
        P("dp", "sector", None, None, None),
        P("dp", "sector", None),
        P("dp", None, None, None),
        P(),
        P(),
        P("dp", "sector", None),
    )
    out_specs = (P("dp", "sector", None), P("dp", "sector", None), P(), P())
    return jax.shard_map(
        per_device, mesh=mesh, in_specs=in_specs, out_specs=out_specs, check_vma=False
    )
```

```python
import jax
import jax.numpy as jnp
from jax import lax
from jax.experimental import pallas as pl
from jax.experimental.pallas import tpu as pltpu
from jax.sharding import PartitionSpec as P

LAYERS = 2
GROUP = 8


def slot_rows(own_ref, lent_ref, slot):
    own = own_ref.shape[0]
    return jnp.where(
        slot < own,
        own_ref[jnp.minimum(slot, own - 1)],
        lent_ref[jnp.maximum(slot - own, 0)],
    )


def layer_kernel(src_ref, tiles_ref, own_ref, lent_ref, hits_ref, weight_ref, pre_ref, out_ref):
    step = pl.program_id(0)
    listed = tiles_ref.shape[1]
    for i in range(GROUP):
        block = step * GROUP + i
        lhs = jnp.concatenate([tiles_ref[i, k] for k in range(listed)], axis=1)
        rhs = jnp.concatenate(
            [slot_rows(own_ref, lent_ref, src_ref[block, k]) for k in range(listed)], axis=0
        )
        rows = hits_ref[i]
        pre = jnp.dot(lhs, rhs, preferred_element_type=jnp.float32) + jnp.dot(
            rows, weight_ref[...], preferred_element_type=jnp.float32
        )
        pre_ref[i] = pre
        out_ref[i] = (rows.astype(jnp.float32) + pre * jax.nn.sigmoid(pre)).astype(
            out_ref.dtype
        )


def block_layer(slot_ids, tile_data, own_table, lent_table, hit_blocks, weight):
    blocks, listed, rows, _ = tile_data.shape
    width = own_table.shape[-1]
    block_spec = pl.BlockSpec((GROUP, rows, width), lambda g, src: (g, 0, 0))
    return pl.pallas_call(
        layer_kernel,
        grid_spec=pltpu.PrefetchScalarGridSpec(
            num_scalar_prefetch=1,
            grid=(blocks // GROUP,),
            in_specs=[
                pl.BlockSpec((GROUP, listed, rows, rows), lambda g, src: (g, 0, 0, 0)),
                pl.BlockSpec(own_table.shape, lambda g, src: (0, 0, 0)),
                pl.BlockSpec(lent_table.shape, lambda g, src: (0, 0, 0)),
                block_spec,
                pl.BlockSpec(weight.shape, lambda g, src: (0, 0)),
            ],
            out_specs=[block_spec, block_spec],
        ),
        out_shape=[
            jax.ShapeDtypeStruct((blocks, rows, width), jnp.float32),
            jax.ShapeDtypeStruct((blocks, rows, width), hit_blocks.dtype),
        ],
    )(slot_ids, tile_data, own_table, lent_table, hit_blocks, weight)


def slot_grad_kernel(src_ref, tiles_ref, grad_ref, pre_ref, own_ref, low_ref, high_ref, dpre_ref, out_ref):
    step = pl.program_id(0)

    @pl.when(step == 0)
    def _():
        out_ref[...] = jnp.zeros(out_ref.shape, out_ref.dtype)

    for i in range(GROUP):
        block = step * GROUP + i
        pre = pre_ref[i]
        sig = jax.nn.sigmoid(pre)
        grad = (grad_ref[i] * (sig * (1.0 + pre * (1.0 - sig)))).astype(dpre_ref.dtype)
        dpre_ref[i] = grad
        for k in range(tiles_ref.shape[1]):
            slot = src_ref[block, k]
            part = lax.dot_general(
                tiles_ref[i, k], grad, (((0,), (0,)), ((), ())),
                preferred_element_type=jnp.float32,
            )
            out_ref[slot] += part

    @pl.when(step == pl.num_programs(0) - 1)
    def _():
        own = own_ref.shape[0]
        lent = low_ref.shape[0]
        own_ref[...] = out_ref[:own]
        low_ref[...] = out_ref[own : own + lent].astype(low_ref.dtype)
        high_ref[...] = out_ref[own + lent :].astype(high_ref.dtype)


def block_slot_grad(slot_ids, tile_data, grad_blocks, pre_blocks, slot_count):
    blocks, listed, rows, _ = tile_data.shape
    width = grad_blocks.shape[-1]
    lent = (slot_count - blocks) // 2
    block_spec = pl.BlockSpec((GROUP, rows, width), lambda g, src: (g, 0, 0))
    whole = lambda count: pl.BlockSpec((count, rows, width), lambda g, src: (0, 0, 0))
    return pl.pallas_call(
        slot_grad_kernel,
        grid_spec=pltpu.PrefetchScalarGridSpec(
            num_scalar_prefetch=1,
            grid=(blocks // GROUP,),
            in_specs=[
                pl.BlockSpec((GROUP, listed, rows, rows), lambda g, src: (g, 0, 0, 0)),
                block_spec,
                block_spec,
            ],
            out_specs=[whole(blocks), whole(lent), whole(lent), block_spec],
            scratch_shapes=[pltpu.VMEM((slot_count, rows, width), jnp.float32)],
        ),
        out_shape=[
            jax.ShapeDtypeStruct((blocks, rows, width), jnp.float32),
            jax.ShapeDtypeStruct((lent, rows, width), jnp.bfloat16),
            jax.ShapeDtypeStruct((lent, rows, width), jnp.bfloat16),
            jax.ShapeDtypeStruct((blocks, rows, width), jnp.bfloat16),
        ],
        compiler_params=pltpu.CompilerParams(dimension_semantics=("arbitrary",)),
    )(slot_ids, tile_data, grad_blocks, pre_blocks)


def fold_kernel(lists_ref, slot_ref, lower_ref, upper_ref, out_ref, acc_ref):
    acc_ref[...] = slot_ref[...]
    for i in range(lower_ref.shape[0]):
        block = lists_ref[1, i]
        acc_ref[block] += lower_ref[i].astype(jnp.float32)
    for i in range(upper_ref.shape[0]):
        block = lists_ref[0, i]
        acc_ref[block] += upper_ref[i].astype(jnp.float32)
    out_ref[...] = acc_ref[...].astype(out_ref.dtype)


def fold_lent(own_lists, slot_grad, from_lower, from_upper, blocks):
    _, rows, width = slot_grad.shape
    lent = from_lower.shape[0]
    return pl.pallas_call(
        fold_kernel,
        grid_spec=pltpu.PrefetchScalarGridSpec(
            num_scalar_prefetch=1,
            grid=(1,),
            in_specs=[
                pl.BlockSpec((blocks, rows, width), lambda g, lists: (0, 0, 0)),
                pl.BlockSpec((lent, rows, width), lambda g, lists: (0, 0, 0)),
                pl.BlockSpec((lent, rows, width), lambda g, lists: (0, 0, 0)),
            ],
            out_specs=pl.BlockSpec((blocks, rows, width), lambda g, lists: (0, 0, 0)),
            scratch_shapes=[pltpu.VMEM((blocks, rows, width), jnp.float32)],
        ),
        out_shape=jax.ShapeDtypeStruct((blocks, rows, width), jnp.bfloat16),
    )(own_lists, slot_grad, from_lower, from_upper)


def to_upper(x, axis):
    count = lax.axis_size(axis)
    return lax.ppermute(x, axis, [(i, (i + 1) % count) for i in range(count)])


def to_lower(x, axis):
    count = lax.axis_size(axis)
    return lax.ppermute(x, axis, [((i + 1) % count, i) for i in range(count)])


def all_reduce(x, axes, scale):
    count = lax.axis_size(axes)
    width = x.shape[-1]
    pieces = x.reshape(count, -1, width)
    mine = lax.all_to_all(pieces, axes, 0, 0, tiled=True).sum(0) * scale
    spread = jnp.broadcast_to(mine[None], (count,) + mine.shape)
    return lax.all_to_all(spread, axes, 0, 0, tiled=True).reshape(x.shape)


def silu_grad(pre):
    sig = jax.nn.sigmoid(pre)
    return sig * (1.0 + pre * (1.0 - sig))


def per_device(hits, tiles, sources, send_list, w_message, w_self, cotangent):
    blocks_here = tiles.shape[1]
    tile_rows = tiles.shape[3]
    width = hits.shape[2]
    lent = send_list.shape[3]
    listed = tiles.shape[2]
    sector_here = lax.axis_index("sector")
    lists = send_list[0]
    own_lists = lax.dynamic_index_in_dim(lists, sector_here, 0, keepdims=False)
    tile_data = tiles[0]
    slot_ids = sources[0]
    slot_count = blocks_here + 2 * lent
    current = hits[0]
    saved = []
    for layer_index in range(LAYERS):
        message = jnp.dot(
            current, w_message[layer_index], preferred_element_type=jnp.float32
        ).astype(jnp.bfloat16)
        message_blocks = message.reshape(blocks_here, tile_rows, width)
        from_lower = to_upper(message_blocks[own_lists[0]], "sector")
        from_upper = to_lower(message_blocks[own_lists[1]], "sector")
        pre, following = block_layer(
            slot_ids, tile_data, message_blocks, jnp.concatenate([from_lower, from_upper]),
            current.reshape(message_blocks.shape),
            w_self[layer_index],
        )
        saved.append((current, pre.reshape(-1, width)))
        current = following.reshape(-1, width)
    grad = cotangent[0]
    message_steps = [None] * LAYERS
    self_steps = [None] * LAYERS
    for layer_index in reversed(range(LAYERS)):
        layer_in, pre = saved[layer_index]
        own_grad, low_grad, high_grad, dpre_blocks = block_slot_grad(
            slot_ids, tile_data, grad.reshape(blocks_here, tile_rows, width),
            pre.reshape(blocks_here, tile_rows, width), slot_count,
        )
        dpre = dpre_blocks.reshape(-1, width)
        lent_down_grad = to_upper(high_grad, "sector")
        lent_up_grad = to_lower(low_grad, "sector")
        dmessage = fold_lent(
            own_lists, own_grad, lent_down_grad, lent_up_grad, blocks_here
        ).reshape(-1, width)
        self_part = jnp.dot(layer_in.T, dpre, preferred_element_type=jnp.float32)
        message_part = jnp.dot(layer_in.T, dmessage, preferred_element_type=jnp.float32)
        message_steps[layer_index] = message_part
        self_steps[layer_index] = self_part
        grad = grad + jnp.dot(dpre, w_self[layer_index].T, preferred_element_type=jnp.float32)
        grad = grad + jnp.dot(
            dmessage, w_message[layer_index].T, preferred_element_type=jnp.float32
        )
    message_total = jnp.stack(message_steps)
    self_total = jnp.stack(self_steps)
    total_rows = blocks_here * tile_rows * lax.axis_size(("dp", "sector"))
    scale = 1.0 / jnp.sqrt(jnp.float32(total_rows))
    both = all_reduce(jnp.stack([message_total, self_total]), ("dp", "sector"), scale)
    return (current[None], grad[None], both[0], both[1])


def solution(mesh):
    in_specs = (
        P("dp", "sector", None),
        P("dp", "sector", None, None, None),
        P("dp", "sector", None),
        P("dp", None, None, None),
        P(),
        P(),
        P("dp", "sector", None),
    )
    out_specs = (P("dp", "sector", None), P("dp", "sector", None), P(), P())
    return jax.shard_map(
        per_device, mesh=mesh, in_specs=in_specs, out_specs=out_specs, check_vma=False
    )
```

```python
import jax
import jax.numpy as jnp
from jax import lax
from jax.experimental import pallas as pl
from jax.experimental.pallas import tpu as pltpu
from jax.sharding import PartitionSpec as P

LAYERS = 2
GROUP = 8


def slot_rows(own_ref, lent_ref, slot):
    own = own_ref.shape[0]
    return jnp.where(
        slot < own,
        own_ref[jnp.minimum(slot, own - 1)],
        lent_ref[jnp.maximum(slot - own, 0)],
    )


def layer_kernel(src_ref, tiles_ref, own_ref, lent_ref, hits_ref, weight_ref, pre_ref, out_ref):
    step = pl.program_id(0)
    listed = tiles_ref.shape[1]
    for i in range(GROUP):
        block = step * GROUP + i
        lhs = jnp.concatenate([tiles_ref[i, k] for k in range(listed)], axis=1)
        rhs = jnp.concatenate(
            [slot_rows(own_ref, lent_ref, src_ref[block, k]) for k in range(listed)], axis=0
        )
        rows = hits_ref[i]
        pre = jnp.dot(lhs, rhs, preferred_element_type=jnp.float32) + jnp.dot(
            rows, weight_ref[...], preferred_element_type=jnp.float32
        )
        pre_ref[i] = pre
        out_ref[i] = (rows.astype(jnp.float32) + pre * jax.nn.sigmoid(pre)).astype(
            out_ref.dtype
        )


def block_layer(slot_ids, tile_data, own_table, lent_table, hit_blocks, weight):
    blocks, listed, rows, _ = tile_data.shape
    width = own_table.shape[-1]
    block_spec = pl.BlockSpec((GROUP, rows, width), lambda g, src: (g, 0, 0))
    return pl.pallas_call(
        layer_kernel,
        grid_spec=pltpu.PrefetchScalarGridSpec(
            num_scalar_prefetch=1,
            grid=(blocks // GROUP,),
            in_specs=[
                pl.BlockSpec((GROUP, listed, rows, rows), lambda g, src: (g, 0, 0, 0)),
                pl.BlockSpec(own_table.shape, lambda g, src: (0, 0, 0)),
                pl.BlockSpec(lent_table.shape, lambda g, src: (0, 0, 0)),
                block_spec,
                pl.BlockSpec(weight.shape, lambda g, src: (0, 0)),
            ],
            out_specs=[block_spec, block_spec],
        ),
        out_shape=[
            jax.ShapeDtypeStruct((blocks, rows, width), jnp.float32),
            jax.ShapeDtypeStruct((blocks, rows, width), hit_blocks.dtype),
        ],
    )(slot_ids, tile_data, own_table, lent_table, hit_blocks, weight)


def slot_grad_kernel(src_ref, tiles_ref, grad_ref, pre_ref, own_ref, low_ref, high_ref, dpre_ref, out_ref):
    step = pl.program_id(0)

    @pl.when(step == 0)
    def _():
        out_ref[...] = jnp.zeros(out_ref.shape, out_ref.dtype)

    for i in range(GROUP):
        block = step * GROUP + i
        pre = pre_ref[i]
        sig = jax.nn.sigmoid(pre)
        grad = (grad_ref[i] * (sig * (1.0 + pre * (1.0 - sig)))).astype(dpre_ref.dtype)
        dpre_ref[i] = grad
        for k in range(tiles_ref.shape[1]):
            slot = src_ref[block, k]
            part = lax.dot_general(
                tiles_ref[i, k], grad, (((0,), (0,)), ((), ())),
                preferred_element_type=jnp.float32,
            )
            out_ref[slot] += part

    @pl.when(step == pl.num_programs(0) - 1)
    def _():
        own = own_ref.shape[0]
        lent = low_ref.shape[0]
        own_ref[...] = out_ref[:own]
        low_ref[...] = out_ref[own : own + lent].astype(low_ref.dtype)
        high_ref[...] = out_ref[own + lent :].astype(high_ref.dtype)


def block_slot_grad(slot_ids, tile_data, grad_blocks, pre_blocks, slot_count):
    blocks, listed, rows, _ = tile_data.shape
    width = grad_blocks.shape[-1]
    lent = (slot_count - blocks) // 2
    block_spec = pl.BlockSpec((GROUP, rows, width), lambda g, src: (g, 0, 0))
    whole = lambda count: pl.BlockSpec((count, rows, width), lambda g, src: (0, 0, 0))
    return pl.pallas_call(
        slot_grad_kernel,
        grid_spec=pltpu.PrefetchScalarGridSpec(
            num_scalar_prefetch=1,
            grid=(blocks // GROUP,),
            in_specs=[
                pl.BlockSpec((GROUP, listed, rows, rows), lambda g, src: (g, 0, 0, 0)),
                block_spec,
                block_spec,
            ],
            out_specs=[whole(blocks), whole(lent), whole(lent), block_spec],
            scratch_shapes=[pltpu.VMEM((slot_count, rows, width), jnp.float32)],
        ),
        out_shape=[
            jax.ShapeDtypeStruct((blocks, rows, width), jnp.float32),
            jax.ShapeDtypeStruct((lent, rows, width), jnp.bfloat16),
            jax.ShapeDtypeStruct((lent, rows, width), jnp.bfloat16),
            jax.ShapeDtypeStruct((blocks, rows, width), jnp.bfloat16),
        ],
        compiler_params=pltpu.CompilerParams(dimension_semantics=("arbitrary",)),
    )(slot_ids, tile_data, grad_blocks, pre_blocks)


FOLD = 4


def fold_kernel(lists_ref, own_ref, lower_ref, upper_ref, out_ref, acc_ref):
    base = pl.program_id(0) * acc_ref.shape[0]
    acc_ref[...] = own_ref[...]
    for list_index, part_ref in ((1, lower_ref), (0, upper_ref)):
        for i in range(part_ref.shape[0]):
            local = lists_ref[list_index, i] - base

            @pl.when((local >= 0) & (local < acc_ref.shape[0]))
            def _():
                acc_ref[local] += part_ref[i].astype(jnp.float32)

    out_ref[...] = acc_ref[...].astype(out_ref.dtype)


def fold_lent(own_lists, slot_grad, from_lower, from_upper, blocks):
    _, rows, width = slot_grad.shape
    lent = from_lower.shape[0]
    step_spec = pl.BlockSpec((FOLD, rows, width), lambda g, lists: (g, 0, 0))
    return pl.pallas_call(
        fold_kernel,
        grid_spec=pltpu.PrefetchScalarGridSpec(
            num_scalar_prefetch=1,
            grid=(blocks // FOLD,),
            in_specs=[
                step_spec,
                pl.BlockSpec((lent, rows, width), lambda g, lists: (0, 0, 0)),
                pl.BlockSpec((lent, rows, width), lambda g, lists: (0, 0, 0)),
            ],
            out_specs=step_spec,
            scratch_shapes=[pltpu.VMEM((FOLD, rows, width), jnp.float32)],
        ),
        out_shape=jax.ShapeDtypeStruct((blocks, rows, width), jnp.bfloat16),
    )(own_lists, slot_grad, from_lower, from_upper)


def to_upper(x, axis):
    count = lax.axis_size(axis)
    return lax.ppermute(x, axis, [(i, (i + 1) % count) for i in range(count)])


def to_lower(x, axis):
    count = lax.axis_size(axis)
    return lax.ppermute(x, axis, [((i + 1) % count, i) for i in range(count)])


def all_reduce(x, axes, scale):
    count = lax.axis_size(axes)
    width = x.shape[-1]
    pieces = x.reshape(count, -1, width)
    mine = lax.all_to_all(pieces, axes, 0, 0, tiled=True).sum(0) * scale
    spread = jnp.broadcast_to(mine[None], (count,) + mine.shape)
    return lax.all_to_all(spread, axes, 0, 0, tiled=True).reshape(x.shape)


def silu_grad(pre):
    sig = jax.nn.sigmoid(pre)
    return sig * (1.0 + pre * (1.0 - sig))


def per_device(hits, tiles, sources, send_list, w_message, w_self, cotangent):
    blocks_here = tiles.shape[1]
    tile_rows = tiles.shape[3]
    width = hits.shape[2]
    lent = send_list.shape[3]
    listed = tiles.shape[2]
    sector_here = lax.axis_index("sector")
    lists = send_list[0]
    own_lists = lax.dynamic_index_in_dim(lists, sector_here, 0, keepdims=False)
    tile_data = tiles[0]
    slot_ids = sources[0]
    slot_count = blocks_here + 2 * lent
    current = hits[0]
    saved = []
    for layer_index in range(LAYERS):
        message = jnp.dot(
            current, w_message[layer_index], preferred_element_type=jnp.float32
        ).astype(jnp.bfloat16)
        message_blocks = message.reshape(blocks_here, tile_rows, width)
        from_lower = to_upper(message_blocks[own_lists[0]], "sector")
        from_upper = to_lower(message_blocks[own_lists[1]], "sector")
        pre, following = block_layer(
            slot_ids, tile_data, message_blocks, jnp.concatenate([from_lower, from_upper]),
            current.reshape(message_blocks.shape),
            w_self[layer_index],
        )
        saved.append((current, pre.reshape(-1, width)))
        current = following.reshape(-1, width)
    grad = cotangent[0]
    message_steps = [None] * LAYERS
    self_steps = [None] * LAYERS
    for layer_index in reversed(range(LAYERS)):
        layer_in, pre = saved[layer_index]
        own_grad, low_grad, high_grad, dpre_blocks = block_slot_grad(
            slot_ids, tile_data, grad.reshape(blocks_here, tile_rows, width),
            pre.reshape(blocks_here, tile_rows, width), slot_count,
        )
        dpre = dpre_blocks.reshape(-1, width)
        lent_down_grad = to_upper(high_grad, "sector")
        lent_up_grad = to_lower(low_grad, "sector")
        dmessage = fold_lent(
            own_lists, own_grad, lent_down_grad, lent_up_grad, blocks_here
        ).reshape(-1, width)
        self_part = jnp.dot(layer_in.T, dpre, preferred_element_type=jnp.float32)
        message_part = jnp.dot(layer_in.T, dmessage, preferred_element_type=jnp.float32)
        message_steps[layer_index] = message_part
        self_steps[layer_index] = self_part
        grad = grad + jnp.dot(dpre, w_self[layer_index].T, preferred_element_type=jnp.float32)
        grad = grad + jnp.dot(
            dmessage, w_message[layer_index].T, preferred_element_type=jnp.float32
        )
    message_total = jnp.stack(message_steps)
    self_total = jnp.stack(self_steps)
    total_rows = blocks_here * tile_rows * lax.axis_size(("dp", "sector"))
    scale = 1.0 / jnp.sqrt(jnp.float32(total_rows))
    both = all_reduce(jnp.stack([message_total, self_total]), ("dp", "sector"), scale)
    return (current[None], grad[None], both[0], both[1])


def solution(mesh):
    in_specs = (
        P("dp", "sector", None),
        P("dp", "sector", None, None, None),
        P("dp", "sector", None),
        P("dp", None, None, None),
        P(),
        P(),
        P("dp", "sector", None),
    )
    out_specs = (P("dp", "sector", None), P("dp", "sector", None), P(), P())
    return jax.shard_map(
        per_device, mesh=mesh, in_specs=in_specs, out_specs=out_specs, check_vma=False
    )
```

```python
import jax
import jax.numpy as jnp
from jax import lax
from jax.experimental import pallas as pl
from jax.experimental.pallas import tpu as pltpu
from jax.sharding import PartitionSpec as P

LAYERS = 2
GROUP = 8


def slot_rows(own_ref, lent_ref, slot):
    own = own_ref.shape[0]
    return jnp.where(
        slot < own,
        own_ref[jnp.minimum(slot, own - 1)],
        lent_ref[jnp.maximum(slot - own, 0)],
    )


def layer_kernel(src_ref, tiles_ref, own_ref, lent_ref, hits_ref, weight_ref, pre_ref, out_ref):
    step = pl.program_id(0)
    listed = tiles_ref.shape[1]
    for i in range(GROUP):
        block = step * GROUP + i
        lhs = jnp.concatenate([tiles_ref[i, k] for k in range(listed)], axis=1)
        rhs = jnp.concatenate(
            [slot_rows(own_ref, lent_ref, src_ref[block, k]) for k in range(listed)], axis=0
        )
        rows = hits_ref[i]
        pre = jnp.dot(lhs, rhs, preferred_element_type=jnp.float32) + jnp.dot(
            rows, weight_ref[...], preferred_element_type=jnp.float32
        )
        pre_ref[i] = pre
        out_ref[i] = (rows.astype(jnp.float32) + pre * jax.nn.sigmoid(pre)).astype(
            out_ref.dtype
        )


def block_layer(slot_ids, tile_data, own_table, lent_table, hit_blocks, weight):
    blocks, listed, rows, _ = tile_data.shape
    width = own_table.shape[-1]
    block_spec = pl.BlockSpec((GROUP, rows, width), lambda g, src: (g, 0, 0))
    return pl.pallas_call(
        layer_kernel,
        grid_spec=pltpu.PrefetchScalarGridSpec(
            num_scalar_prefetch=1,
            grid=(blocks // GROUP,),
            in_specs=[
                pl.BlockSpec((GROUP, listed, rows, rows), lambda g, src: (g, 0, 0, 0)),
                pl.BlockSpec(own_table.shape, lambda g, src: (0, 0, 0)),
                pl.BlockSpec(lent_table.shape, lambda g, src: (0, 0, 0)),
                block_spec,
                pl.BlockSpec(weight.shape, lambda g, src: (0, 0)),
            ],
            out_specs=[block_spec, block_spec],
        ),
        out_shape=[
            jax.ShapeDtypeStruct((blocks, rows, width), jnp.float32),
            jax.ShapeDtypeStruct((blocks, rows, width), hit_blocks.dtype),
        ],
    )(slot_ids, tile_data, own_table, lent_table, hit_blocks, weight)


def slot_grad_kernel(src_ref, tiles_ref, grad_ref, pre_ref, own_ref, low_ref, high_ref, dpre_ref, out_ref):
    step = pl.program_id(0)

    @pl.when(step == 0)
    def _():
        out_ref[...] = jnp.zeros(out_ref.shape, out_ref.dtype)

    for i in range(GROUP):
        block = step * GROUP + i
        pre = pre_ref[i]
        sig = jax.nn.sigmoid(pre)
        grad = (grad_ref[i] * (sig * (1.0 + pre * (1.0 - sig)))).astype(dpre_ref.dtype)
        dpre_ref[i] = grad
        for k in range(tiles_ref.shape[1]):
            slot = src_ref[block, k]
            part = lax.dot_general(
                tiles_ref[i, k], grad, (((0,), (0,)), ((), ())),
                preferred_element_type=jnp.float32,
            )
            out_ref[slot] += part

    @pl.when(step == pl.num_programs(0) - 1)
    def _():
        own = own_ref.shape[0]
        lent = low_ref.shape[0]
        own_ref[...] = out_ref[:own]
        low_ref[...] = out_ref[own : own + lent].astype(low_ref.dtype)
        high_ref[...] = out_ref[own + lent :].astype(high_ref.dtype)


def block_slot_grad(slot_ids, tile_data, grad_blocks, pre_blocks, slot_count):
    blocks, listed, rows, _ = tile_data.shape
    width = grad_blocks.shape[-1]
    lent = (slot_count - blocks) // 2
    block_spec = pl.BlockSpec((GROUP, rows, width), lambda g, src: (g, 0, 0))
    whole = lambda count: pl.BlockSpec((count, rows, width), lambda g, src: (0, 0, 0))
    return pl.pallas_call(
        slot_grad_kernel,
        grid_spec=pltpu.PrefetchScalarGridSpec(
            num_scalar_prefetch=1,
            grid=(blocks // GROUP,),
            in_specs=[
                pl.BlockSpec((GROUP, listed, rows, rows), lambda g, src: (g, 0, 0, 0)),
                block_spec,
                block_spec,
            ],
            out_specs=[whole(blocks), whole(lent), whole(lent), block_spec],
            scratch_shapes=[pltpu.VMEM((slot_count, rows, width), jnp.float32)],
        ),
        out_shape=[
            jax.ShapeDtypeStruct((blocks, rows, width), jnp.float32),
            jax.ShapeDtypeStruct((lent, rows, width), jnp.bfloat16),
            jax.ShapeDtypeStruct((lent, rows, width), jnp.bfloat16),
            jax.ShapeDtypeStruct((blocks, rows, width), jnp.bfloat16),
        ],
        compiler_params=pltpu.CompilerParams(dimension_semantics=("arbitrary",)),
    )(slot_ids, tile_data, grad_blocks, pre_blocks)


def fold_kernel(lists_ref, slot_ref, lower_ref, upper_ref, out_ref, acc_ref):
    acc_ref[...] = slot_ref[...]
    for i in range(lower_ref.shape[0]):
        block = lists_ref[1, i]
        acc_ref[block] += lower_ref[i].astype(jnp.float32)
    for i in range(upper_ref.shape[0]):
        block = lists_ref[0, i]
        acc_ref[block] += upper_ref[i].astype(jnp.float32)
    out_ref[...] = acc_ref[...].astype(out_ref.dtype)


def fold_lent(own_lists, slot_grad, from_lower, from_upper, blocks):
    _, rows, width = slot_grad.shape
    lent = from_lower.shape[0]
    return pl.pallas_call(
        fold_kernel,
        grid_spec=pltpu.PrefetchScalarGridSpec(
            num_scalar_prefetch=1,
            grid=(1,),
            in_specs=[
                pl.BlockSpec((blocks, rows, width), lambda g, lists: (0, 0, 0)),
                pl.BlockSpec((lent, rows, width), lambda g, lists: (0, 0, 0)),
                pl.BlockSpec((lent, rows, width), lambda g, lists: (0, 0, 0)),
            ],
            out_specs=pl.BlockSpec((blocks, rows, width), lambda g, lists: (0, 0, 0)),
            scratch_shapes=[pltpu.VMEM((blocks, rows, width), jnp.float32)],
        ),
        out_shape=jax.ShapeDtypeStruct((blocks, rows, width), jnp.bfloat16),
    )(own_lists, slot_grad, from_lower, from_upper)


def to_upper(x, axis):
    count = lax.axis_size(axis)
    return lax.ppermute(x, axis, [(i, (i + 1) % count) for i in range(count)])


def to_lower(x, axis):
    count = lax.axis_size(axis)
    return lax.ppermute(x, axis, [((i + 1) % count, i) for i in range(count)])


def all_reduce(x, axes, scale):
    count = lax.axis_size(axes)
    width = x.shape[-1]
    pieces = x.reshape(count, -1, width).astype(jnp.bfloat16)
    received = lax.all_to_all(pieces, axes, 0, 0, tiled=True)
    mine = (received.astype(jnp.float32).sum(0) * scale).astype(jnp.bfloat16)
    spread = jnp.broadcast_to(mine[None], (count,) + mine.shape)
    gathered = lax.all_to_all(spread, axes, 0, 0, tiled=True)
    return gathered.astype(jnp.float32).reshape(x.shape)


def silu_grad(pre):
    sig = jax.nn.sigmoid(pre)
    return sig * (1.0 + pre * (1.0 - sig))


def per_device(hits, tiles, sources, send_list, w_message, w_self, cotangent):
    blocks_here = tiles.shape[1]
    tile_rows = tiles.shape[3]
    width = hits.shape[2]
    lent = send_list.shape[3]
    listed = tiles.shape[2]
    sector_here = lax.axis_index("sector")
    lists = send_list[0]
    own_lists = lax.dynamic_index_in_dim(lists, sector_here, 0, keepdims=False)
    tile_data = tiles[0]
    slot_ids = sources[0]
    slot_count = blocks_here + 2 * lent
    current = hits[0]
    saved = []
    for layer_index in range(LAYERS):
        message = jnp.dot(
            current, w_message[layer_index], preferred_element_type=jnp.float32
        ).astype(jnp.bfloat16)
        message_blocks = message.reshape(blocks_here, tile_rows, width)
        from_lower = to_upper(message_blocks[own_lists[0]], "sector")
        from_upper = to_lower(message_blocks[own_lists[1]], "sector")
        pre, following = block_layer(
            slot_ids, tile_data, message_blocks, jnp.concatenate([from_lower, from_upper]),
            current.reshape(message_blocks.shape),
            w_self[layer_index],
        )
        saved.append((current, pre.reshape(-1, width)))
        current = following.reshape(-1, width)
    grad = cotangent[0]
    message_steps = [None] * LAYERS
    self_steps = [None] * LAYERS
    for layer_index in reversed(range(LAYERS)):
        layer_in, pre = saved[layer_index]
        own_grad, low_grad, high_grad, dpre_blocks = block_slot_grad(
            slot_ids, tile_data, grad.reshape(blocks_here, tile_rows, width),
            pre.reshape(blocks_here, tile_rows, width), slot_count,
        )
        dpre = dpre_blocks.reshape(-1, width)
        lent_down_grad = to_upper(high_grad, "sector")
        lent_up_grad = to_lower(low_grad, "sector")
        dmessage = fold_lent(
            own_lists, own_grad, lent_down_grad, lent_up_grad, blocks_here
        ).reshape(-1, width)
        self_part = jnp.dot(layer_in.T, dpre, preferred_element_type=jnp.float32)
        message_part = jnp.dot(layer_in.T, dmessage, preferred_element_type=jnp.float32)
        message_steps[layer_index] = message_part
        self_steps[layer_index] = self_part
        grad = grad + jnp.dot(dpre, w_self[layer_index].T, preferred_element_type=jnp.float32)
        grad = grad + jnp.dot(
            dmessage, w_message[layer_index].T, preferred_element_type=jnp.float32
        )
    message_total = jnp.stack(message_steps)
    self_total = jnp.stack(self_steps)
    total_rows = blocks_here * tile_rows * lax.axis_size(("dp", "sector"))
    scale = 1.0 / jnp.sqrt(jnp.float32(total_rows))
    both = all_reduce(jnp.stack([message_total, self_total]), ("dp", "sector"), scale)
    return (current[None], grad[None], both[0], both[1])


def solution(mesh):
    in_specs = (
        P("dp", "sector", None),
        P("dp", "sector", None, None, None),
        P("dp", "sector", None),
        P("dp", None, None, None),
        P(),
        P(),
        P("dp", "sector", None),
    )
    out_specs = (P("dp", "sector", None), P("dp", "sector", None), P(), P())
    return jax.shard_map(
        per_device, mesh=mesh, in_specs=in_specs, out_specs=out_specs, check_vma=False
    )
```

```python
import jax
import jax.numpy as jnp
from jax import lax
from jax.experimental import pallas as pl
from jax.experimental.pallas import tpu as pltpu
from jax.sharding import PartitionSpec as P

LAYERS = 2
GROUP = 8
GROUP_BACK = 4


def slot_rows(own_ref, lent_ref, slot):
    own = own_ref.shape[0]
    return jnp.where(
        slot < own,
        own_ref[jnp.minimum(slot, own - 1)],
        lent_ref[jnp.maximum(slot - own, 0)],
    )


def layer_kernel(src_ref, tiles_ref, own_ref, lent_ref, hits_ref, weight_ref, pre_ref, out_ref):
    step = pl.program_id(0)
    listed = tiles_ref.shape[1]
    for i in range(GROUP):
        block = step * GROUP + i
        lhs = jnp.concatenate([tiles_ref[i, k] for k in range(listed)], axis=1)
        rhs = jnp.concatenate(
            [slot_rows(own_ref, lent_ref, src_ref[block, k]) for k in range(listed)], axis=0
        )
        rows = hits_ref[i]
        pre = jnp.dot(lhs, rhs, preferred_element_type=jnp.float32) + jnp.dot(
            rows, weight_ref[...], preferred_element_type=jnp.float32
        )
        pre_ref[i] = pre
        out_ref[i] = (rows.astype(jnp.float32) + pre * jax.nn.sigmoid(pre)).astype(
            out_ref.dtype
        )


def block_layer(slot_ids, tile_data, own_table, lent_table, hit_blocks, weight):
    blocks, listed, rows, _ = tile_data.shape
    width = own_table.shape[-1]
    block_spec = pl.BlockSpec((GROUP, rows, width), lambda g, src: (g, 0, 0))
    return pl.pallas_call(
        layer_kernel,
        grid_spec=pltpu.PrefetchScalarGridSpec(
            num_scalar_prefetch=1,
            grid=(blocks // GROUP,),
            in_specs=[
                pl.BlockSpec((GROUP, listed, rows, rows), lambda g, src: (g, 0, 0, 0)),
                pl.BlockSpec(own_table.shape, lambda g, src: (0, 0, 0)),
                pl.BlockSpec(lent_table.shape, lambda g, src: (0, 0, 0)),
                block_spec,
                pl.BlockSpec(weight.shape, lambda g, src: (0, 0)),
            ],
            out_specs=[block_spec, block_spec],
        ),
        out_shape=[
            jax.ShapeDtypeStruct((blocks, rows, width), jnp.float32),
            jax.ShapeDtypeStruct((blocks, rows, width), hit_blocks.dtype),
        ],
    )(slot_ids, tile_data, own_table, lent_table, hit_blocks, weight)


def slot_grad_kernel(src_ref, tiles_ref, grad_ref, pre_ref, own_ref, low_ref, high_ref, dpre_ref, out_ref):
    step = pl.program_id(0)

    @pl.when(step == 0)
    def _():
        out_ref[...] = jnp.zeros(out_ref.shape, out_ref.dtype)

    group = tiles_ref.shape[0]
    for i in range(group):
        block = step * group + i
        pre = pre_ref[i]
        sig = jax.nn.sigmoid(pre)
        grad = (grad_ref[i] * (sig * (1.0 + pre * (1.0 - sig)))).astype(dpre_ref.dtype)
        dpre_ref[i] = grad
        for k in range(tiles_ref.shape[1]):
            slot = src_ref[block, k]
            part = lax.dot_general(
                tiles_ref[i, k], grad, (((0,), (0,)), ((), ())),
                preferred_element_type=jnp.float32,
            )
            out_ref[slot] += part

    @pl.when(step == pl.num_programs(0) - 1)
    def _():
        own = own_ref.shape[0]
        lent = low_ref.shape[0]
        own_ref[...] = out_ref[:own]
        low_ref[...] = out_ref[own : own + lent].astype(low_ref.dtype)
        high_ref[...] = out_ref[own + lent :].astype(high_ref.dtype)


def block_slot_grad(slot_ids, tile_data, grad_blocks, pre_blocks, slot_count):
    blocks, listed, rows, _ = tile_data.shape
    width = grad_blocks.shape[-1]
    lent = (slot_count - blocks) // 2
    block_spec = pl.BlockSpec((GROUP_BACK, rows, width), lambda g, src: (g, 0, 0))
    whole = lambda count: pl.BlockSpec((count, rows, width), lambda g, src: (0, 0, 0))
    return pl.pallas_call(
        slot_grad_kernel,
        grid_spec=pltpu.PrefetchScalarGridSpec(
            num_scalar_prefetch=1,
            grid=(blocks // GROUP_BACK,),
            in_specs=[
                pl.BlockSpec((GROUP_BACK, listed, rows, rows), lambda g, src: (g, 0, 0, 0)),
                block_spec,
                block_spec,
            ],
            out_specs=[whole(blocks), whole(lent), whole(lent), block_spec],
            scratch_shapes=[pltpu.VMEM((slot_count, rows, width), jnp.float32)],
        ),
        out_shape=[
            jax.ShapeDtypeStruct((blocks, rows, width), jnp.float32),
            jax.ShapeDtypeStruct((lent, rows, width), jnp.bfloat16),
            jax.ShapeDtypeStruct((lent, rows, width), jnp.bfloat16),
            jax.ShapeDtypeStruct((blocks, rows, width), jnp.bfloat16),
        ],
        compiler_params=pltpu.CompilerParams(dimension_semantics=("arbitrary",)),
    )(slot_ids, tile_data, grad_blocks, pre_blocks)


def fold_kernel(lists_ref, slot_ref, lower_ref, upper_ref, out_ref, acc_ref):
    acc_ref[...] = slot_ref[...]
    for i in range(lower_ref.shape[0]):
        block = lists_ref[1, i]
        acc_ref[block] += lower_ref[i].astype(jnp.float32)
    for i in range(upper_ref.shape[0]):
        block = lists_ref[0, i]
        acc_ref[block] += upper_ref[i].astype(jnp.float32)
    out_ref[...] = acc_ref[...].astype(out_ref.dtype)


def fold_lent(own_lists, slot_grad, from_lower, from_upper, blocks):
    _, rows, width = slot_grad.shape
    lent = from_lower.shape[0]
    return pl.pallas_call(
        fold_kernel,
        grid_spec=pltpu.PrefetchScalarGridSpec(
            num_scalar_prefetch=1,
            grid=(1,),
            in_specs=[
                pl.BlockSpec((blocks, rows, width), lambda g, lists: (0, 0, 0)),
                pl.BlockSpec((lent, rows, width), lambda g, lists: (0, 0, 0)),
                pl.BlockSpec((lent, rows, width), lambda g, lists: (0, 0, 0)),
            ],
            out_specs=pl.BlockSpec((blocks, rows, width), lambda g, lists: (0, 0, 0)),
            scratch_shapes=[pltpu.VMEM((blocks, rows, width), jnp.float32)],
        ),
        out_shape=jax.ShapeDtypeStruct((blocks, rows, width), jnp.bfloat16),
    )(own_lists, slot_grad, from_lower, from_upper)


def to_upper(x, axis):
    count = lax.axis_size(axis)
    return lax.ppermute(x, axis, [(i, (i + 1) % count) for i in range(count)])


def to_lower(x, axis):
    count = lax.axis_size(axis)
    return lax.ppermute(x, axis, [((i + 1) % count, i) for i in range(count)])


def all_reduce(x, axes, scale):
    count = lax.axis_size(axes)
    width = x.shape[-1]
    pieces = x.reshape(count, -1, width).astype(jnp.bfloat16)
    received = lax.all_to_all(pieces, axes, 0, 0, tiled=True)
    mine = (received.astype(jnp.float32).sum(0) * scale).astype(jnp.bfloat16)
    spread = jnp.broadcast_to(mine[None], (count,) + mine.shape)
    gathered = lax.all_to_all(spread, axes, 0, 0, tiled=True)
    return gathered.astype(jnp.float32).reshape(x.shape)


def silu_grad(pre):
    sig = jax.nn.sigmoid(pre)
    return sig * (1.0 + pre * (1.0 - sig))


def per_device(hits, tiles, sources, send_list, w_message, w_self, cotangent):
    blocks_here = tiles.shape[1]
    tile_rows = tiles.shape[3]
    width = hits.shape[2]
    lent = send_list.shape[3]
    listed = tiles.shape[2]
    sector_here = lax.axis_index("sector")
    lists = send_list[0]
    own_lists = lax.dynamic_index_in_dim(lists, sector_here, 0, keepdims=False)
    tile_data = tiles[0]
    slot_ids = sources[0]
    slot_count = blocks_here + 2 * lent
    current = hits[0]
    saved = []
    for layer_index in range(LAYERS):
        message = jnp.dot(
            current, w_message[layer_index], preferred_element_type=jnp.float32
        ).astype(jnp.bfloat16)
        message_blocks = message.reshape(blocks_here, tile_rows, width)
        from_lower = to_upper(message_blocks[own_lists[0]], "sector")
        from_upper = to_lower(message_blocks[own_lists[1]], "sector")
        pre, following = block_layer(
            slot_ids, tile_data, message_blocks, jnp.concatenate([from_lower, from_upper]),
            current.reshape(message_blocks.shape),
            w_self[layer_index],
        )
        saved.append((current, pre.reshape(-1, width)))
        current = following.reshape(-1, width)
    grad = cotangent[0]
    message_steps = [None] * LAYERS
    self_steps = [None] * LAYERS
    for layer_index in reversed(range(LAYERS)):
        layer_in, pre = saved[layer_index]
        own_grad, low_grad, high_grad, dpre_blocks = block_slot_grad(
            slot_ids, tile_data, grad.reshape(blocks_here, tile_rows, width),
            pre.reshape(blocks_here, tile_rows, width), slot_count,
        )
        dpre = dpre_blocks.reshape(-1, width)
        lent_down_grad = to_upper(high_grad, "sector")
        lent_up_grad = to_lower(low_grad, "sector")
        dmessage = fold_lent(
            own_lists, own_grad, lent_down_grad, lent_up_grad, blocks_here
        ).reshape(-1, width)
        self_part = jnp.dot(layer_in.T, dpre, preferred_element_type=jnp.float32)
        message_part = jnp.dot(layer_in.T, dmessage, preferred_element_type=jnp.float32)
        message_steps[layer_index] = message_part
        self_steps[layer_index] = self_part
        grad = grad + jnp.dot(dpre, w_self[layer_index].T, preferred_element_type=jnp.float32)
        grad = grad + jnp.dot(
            dmessage, w_message[layer_index].T, preferred_element_type=jnp.float32
        )
    message_total = jnp.stack(message_steps)
    self_total = jnp.stack(self_steps)
    total_rows = blocks_here * tile_rows * lax.axis_size(("dp", "sector"))
    scale = 1.0 / jnp.sqrt(jnp.float32(total_rows))
    both = all_reduce(jnp.stack([message_total, self_total]), ("dp", "sector"), scale)
    return (current[None], grad[None], both[0], both[1])


def solution(mesh):
    in_specs = (
        P("dp", "sector", None),
        P("dp", "sector", None, None, None),
        P("dp", "sector", None),
        P("dp", None, None, None),
        P(),
        P(),
        P("dp", "sector", None),
    )
    out_specs = (P("dp", "sector", None), P("dp", "sector", None), P(), P())
    return jax.shard_map(
        per_device, mesh=mesh, in_specs=in_specs, out_specs=out_specs, check_vma=False
    )
```

```python
import jax
import jax.numpy as jnp
from jax import lax
from jax.experimental import pallas as pl
from jax.experimental.pallas import tpu as pltpu
from jax.sharding import PartitionSpec as P

LAYERS = 2
GROUP = 8


def slot_rows(own_ref, lent_ref, slot):
    own = own_ref.shape[0]
    return jnp.where(
        slot < own,
        own_ref[jnp.minimum(slot, own - 1)],
        lent_ref[jnp.maximum(slot - own, 0)],
    )


def layer_kernel(src_ref, tiles_ref, own_ref, lent_ref, hits_ref, weight_ref, pre_ref, out_ref):
    step = pl.program_id(0)
    listed = tiles_ref.shape[1]
    for i in range(GROUP):
        block = step * GROUP + i
        lhs = jnp.concatenate([tiles_ref[i, k] for k in range(listed)], axis=1)
        rhs = jnp.concatenate(
            [slot_rows(own_ref, lent_ref, src_ref[block, k]) for k in range(listed)], axis=0
        )
        rows = hits_ref[i]
        pre = jnp.dot(lhs, rhs, preferred_element_type=jnp.float32) + jnp.dot(
            rows, weight_ref[...], preferred_element_type=jnp.float32
        )
        pre_ref[i] = pre
        out_ref[i] = (rows.astype(jnp.float32) + pre * jax.nn.sigmoid(pre)).astype(
            out_ref.dtype
        )


def block_layer(slot_ids, tile_data, own_table, lent_table, hit_blocks, weight):
    blocks, listed, rows, _ = tile_data.shape
    width = own_table.shape[-1]
    block_spec = pl.BlockSpec((GROUP, rows, width), lambda g, src: (g, 0, 0))
    return pl.pallas_call(
        layer_kernel,
        grid_spec=pltpu.PrefetchScalarGridSpec(
            num_scalar_prefetch=1,
            grid=(blocks // GROUP,),
            in_specs=[
                pl.BlockSpec((GROUP, listed, rows, rows), lambda g, src: (g, 0, 0, 0)),
                pl.BlockSpec(own_table.shape, lambda g, src: (0, 0, 0)),
                pl.BlockSpec(lent_table.shape, lambda g, src: (0, 0, 0)),
                block_spec,
                pl.BlockSpec(weight.shape, lambda g, src: (0, 0)),
            ],
            out_specs=[block_spec, block_spec],
        ),
        out_shape=[
            jax.ShapeDtypeStruct((blocks, rows, width), jnp.float32),
            jax.ShapeDtypeStruct((blocks, rows, width), hit_blocks.dtype),
        ],
    )(slot_ids, tile_data, own_table, lent_table, hit_blocks, weight)


def slot_grad_kernel(src_ref, tiles_ref, grad_ref, pre_ref, own_ref, low_ref, high_ref, dpre_ref, out_ref):
    step = pl.program_id(0)

    @pl.when(step == 0)
    def _():
        out_ref[...] = jnp.zeros(out_ref.shape, out_ref.dtype)

    for i in range(GROUP):
        block = step * GROUP + i
        pre = pre_ref[i]
        sig = jax.nn.sigmoid(pre)
        grad = (grad_ref[i] * (sig * (1.0 + pre * (1.0 - sig)))).astype(dpre_ref.dtype)
        dpre_ref[i] = grad
        for k in range(tiles_ref.shape[1]):
            slot = src_ref[block, k]
            part = lax.dot_general(
                tiles_ref[i, k], grad, (((0,), (0,)), ((), ())),
                preferred_element_type=jnp.float32,
            )
            out_ref[slot] += part

    @pl.when(step == pl.num_programs(0) - 1)
    def _():
        own = own_ref.shape[0]
        lent = low_ref.shape[0]
        own_ref[...] = out_ref[:own]
        low_ref[...] = out_ref[own : own + lent].astype(low_ref.dtype)
        high_ref[...] = out_ref[own + lent :].astype(high_ref.dtype)


def block_slot_grad(slot_ids, tile_data, grad_blocks, pre_blocks, slot_count):
    blocks, listed, rows, _ = tile_data.shape
    width = grad_blocks.shape[-1]
    lent = (slot_count - blocks) // 2
    block_spec = pl.BlockSpec((GROUP, rows, width), lambda g, src: (g, 0, 0))
    whole = lambda count: pl.BlockSpec((count, rows, width), lambda g, src: (0, 0, 0))
    return pl.pallas_call(
        slot_grad_kernel,
        grid_spec=pltpu.PrefetchScalarGridSpec(
            num_scalar_prefetch=1,
            grid=(blocks // GROUP,),
            in_specs=[
                pl.BlockSpec((GROUP, listed, rows, rows), lambda g, src: (g, 0, 0, 0)),
                block_spec,
                block_spec,
            ],
            out_specs=[whole(blocks), whole(lent), whole(lent), block_spec],
            scratch_shapes=[pltpu.VMEM((slot_count, rows, width), jnp.float32)],
        ),
        out_shape=[
            jax.ShapeDtypeStruct((blocks, rows, width), jnp.float32),
            jax.ShapeDtypeStruct((lent, rows, width), jnp.bfloat16),
            jax.ShapeDtypeStruct((lent, rows, width), jnp.bfloat16),
            jax.ShapeDtypeStruct((blocks, rows, width), jnp.bfloat16),
        ],
        compiler_params=pltpu.CompilerParams(dimension_semantics=("arbitrary",)),
    )(slot_ids, tile_data, grad_blocks, pre_blocks)


def fold_kernel(lists_ref, slot_ref, lower_ref, upper_ref, rows_ref, out_ref, step_ref, acc_ref):
    acc_ref[...] = slot_ref[...]
    for i in range(lower_ref.shape[0]):
        block = lists_ref[1, i]
        acc_ref[block] += lower_ref[i].astype(jnp.float32)
    for i in range(upper_ref.shape[0]):
        block = lists_ref[0, i]
        acc_ref[block] += upper_ref[i].astype(jnp.float32)
    total = None
    for block in range(acc_ref.shape[0]):
        grad = acc_ref[block].astype(out_ref.dtype)
        out_ref[block] = grad
        part = lax.dot_general(
            rows_ref[block], grad, (((0,), (0,)), ((), ())),
            preferred_element_type=jnp.float32,
        )
        total = part if total is None else total + part
    step_ref[...] = total


def fold_lent(own_lists, slot_grad, from_lower, from_upper, row_blocks):
    blocks, rows, width = slot_grad.shape
    lent = from_lower.shape[0]
    whole = lambda count: pl.BlockSpec((count, rows, width), lambda g, lists: (0, 0, 0))
    return pl.pallas_call(
        fold_kernel,
        grid_spec=pltpu.PrefetchScalarGridSpec(
            num_scalar_prefetch=1,
            grid=(1,),
            in_specs=[whole(blocks), whole(lent), whole(lent), whole(blocks)],
            out_specs=[
                whole(blocks),
                pl.BlockSpec((width, width), lambda g, lists: (0, 0)),
            ],
            scratch_shapes=[pltpu.VMEM((blocks, rows, width), jnp.float32)],
        ),
        out_shape=[
            jax.ShapeDtypeStruct((blocks, rows, width), jnp.bfloat16),
            jax.ShapeDtypeStruct((width, width), jnp.float32),
        ],
    )(own_lists, slot_grad, from_lower, from_upper, row_blocks)


def to_upper(x, axis):
    count = lax.axis_size(axis)
    return lax.ppermute(x, axis, [(i, (i + 1) % count) for i in range(count)])


def to_lower(x, axis):
    count = lax.axis_size(axis)
    return lax.ppermute(x, axis, [((i + 1) % count, i) for i in range(count)])


def all_reduce(x, axes, scale):
    count = lax.axis_size(axes)
    width = x.shape[-1]
    pieces = x.reshape(count, -1, width).astype(jnp.bfloat16)
    received = lax.all_to_all(pieces, axes, 0, 0, tiled=True)
    mine = (received.astype(jnp.float32).sum(0) * scale).astype(jnp.bfloat16)
    spread = jnp.broadcast_to(mine[None], (count,) + mine.shape)
    gathered = lax.all_to_all(spread, axes, 0, 0, tiled=True)
    return gathered.astype(jnp.float32).reshape(x.shape)


def silu_grad(pre):
    sig = jax.nn.sigmoid(pre)
    return sig * (1.0 + pre * (1.0 - sig))


def per_device(hits, tiles, sources, send_list, w_message, w_self, cotangent):
    blocks_here = tiles.shape[1]
    tile_rows = tiles.shape[3]
    width = hits.shape[2]
    lent = send_list.shape[3]
    listed = tiles.shape[2]
    sector_here = lax.axis_index("sector")
    lists = send_list[0]
    own_lists = lax.dynamic_index_in_dim(lists, sector_here, 0, keepdims=False)
    tile_data = tiles[0]
    slot_ids = sources[0]
    slot_count = blocks_here + 2 * lent
    current = hits[0]
    saved = []
    for layer_index in range(LAYERS):
        message = jnp.dot(
            current, w_message[layer_index], preferred_element_type=jnp.float32
        ).astype(jnp.bfloat16)
        message_blocks = message.reshape(blocks_here, tile_rows, width)
        from_lower = to_upper(message_blocks[own_lists[0]], "sector")
        from_upper = to_lower(message_blocks[own_lists[1]], "sector")
        pre, following = block_layer(
            slot_ids, tile_data, message_blocks, jnp.concatenate([from_lower, from_upper]),
            current.reshape(message_blocks.shape),
            w_self[layer_index],
        )
        saved.append((current, pre.reshape(-1, width)))
        current = following.reshape(-1, width)
    grad = cotangent[0]
    message_steps = [None] * LAYERS
    self_steps = [None] * LAYERS
    for layer_index in reversed(range(LAYERS)):
        layer_in, pre = saved[layer_index]
        own_grad, low_grad, high_grad, dpre_blocks = block_slot_grad(
            slot_ids, tile_data, grad.reshape(blocks_here, tile_rows, width),
            pre.reshape(blocks_here, tile_rows, width), slot_count,
        )
        dpre = dpre_blocks.reshape(-1, width)
        lent_down_grad = to_upper(high_grad, "sector")
        lent_up_grad = to_lower(low_grad, "sector")
        dmessage, message_part = fold_lent(
            own_lists, own_grad, lent_down_grad, lent_up_grad,
            layer_in.reshape(blocks_here, tile_rows, width),
        )
        dmessage = dmessage.reshape(-1, width)
        self_part = jnp.dot(layer_in.T, dpre, preferred_element_type=jnp.float32)
        message_steps[layer_index] = message_part
        self_steps[layer_index] = self_part
        grad = grad + jnp.dot(dpre, w_self[layer_index].T, preferred_element_type=jnp.float32)
        grad = grad + jnp.dot(
            dmessage, w_message[layer_index].T, preferred_element_type=jnp.float32
        )
    message_total = jnp.stack(message_steps)
    self_total = jnp.stack(self_steps)
    total_rows = blocks_here * tile_rows * lax.axis_size(("dp", "sector"))
    scale = 1.0 / jnp.sqrt(jnp.float32(total_rows))
    both = all_reduce(jnp.stack([message_total, self_total]), ("dp", "sector"), scale)
    return (current[None], grad[None], both[0], both[1])


def solution(mesh):
    in_specs = (
        P("dp", "sector", None),
        P("dp", "sector", None, None, None),
        P("dp", "sector", None),
        P("dp", None, None, None),
        P(),
        P(),
        P("dp", "sector", None),
    )
    out_specs = (P("dp", "sector", None), P("dp", "sector", None), P(), P())
    return jax.shard_map(
        per_device, mesh=mesh, in_specs=in_specs, out_specs=out_specs, check_vma=False
    )
```

```python
import jax
import jax.numpy as jnp
from jax import lax
from jax.experimental import pallas as pl
from jax.experimental.pallas import tpu as pltpu
from jax.sharding import PartitionSpec as P

LAYERS = 2
GROUP = 8


def slot_rows(own_ref, lent_ref, slot):
    own = own_ref.shape[0]
    return jnp.where(
        slot < own,
        own_ref[jnp.minimum(slot, own - 1)],
        lent_ref[jnp.maximum(slot - own, 0)],
    )


def layer_kernel(src_ref, tiles_ref, own_ref, lent_ref, hits_ref, weight_ref, pre_ref, out_ref):
    step = pl.program_id(0)
    listed = tiles_ref.shape[1]
    for i in range(GROUP):
        block = step * GROUP + i
        lhs = jnp.concatenate([tiles_ref[i, k] for k in range(listed)], axis=1)
        rhs = jnp.concatenate(
            [slot_rows(own_ref, lent_ref, src_ref[block, k]) for k in range(listed)], axis=0
        )
        rows = hits_ref[i]
        pre = jnp.dot(lhs, rhs, preferred_element_type=jnp.float32) + jnp.dot(
            rows, weight_ref[...], preferred_element_type=jnp.float32
        )
        pre_ref[i] = pre
        out_ref[i] = (rows.astype(jnp.float32) + pre * jax.nn.sigmoid(pre)).astype(
            out_ref.dtype
        )


def block_layer(slot_ids, tile_data, own_table, lent_table, hit_blocks, weight):
    blocks, listed, rows, _ = tile_data.shape
    width = own_table.shape[-1]
    block_spec = pl.BlockSpec((GROUP, rows, width), lambda g, src: (g, 0, 0))
    return pl.pallas_call(
        layer_kernel,
        grid_spec=pltpu.PrefetchScalarGridSpec(
            num_scalar_prefetch=1,
            grid=(blocks // GROUP,),
            in_specs=[
                pl.BlockSpec((GROUP, listed, rows, rows), lambda g, src: (g, 0, 0, 0)),
                pl.BlockSpec(own_table.shape, lambda g, src: (0, 0, 0)),
                pl.BlockSpec(lent_table.shape, lambda g, src: (0, 0, 0)),
                block_spec,
                pl.BlockSpec(weight.shape, lambda g, src: (0, 0)),
            ],
            out_specs=[block_spec, block_spec],
        ),
        out_shape=[
            jax.ShapeDtypeStruct((blocks, rows, width), jnp.float32),
            jax.ShapeDtypeStruct((blocks, rows, width), hit_blocks.dtype),
        ],
    )(slot_ids, tile_data, own_table, lent_table, hit_blocks, weight)


def slot_grad_kernel(src_ref, tiles_ref, grad_ref, pre_ref, own_ref, low_ref, high_ref, dpre_ref, out_ref):
    step = pl.program_id(0)

    @pl.when(step == 0)
    def _():
        out_ref[...] = jnp.zeros(out_ref.shape, out_ref.dtype)

    for i in range(GROUP):
        block = step * GROUP + i
        pre = pre_ref[i]
        sig = jax.nn.sigmoid(pre)
        grad = (grad_ref[i] * (sig * (1.0 + pre * (1.0 - sig)))).astype(dpre_ref.dtype)
        dpre_ref[i] = grad
        for k in range(tiles_ref.shape[1]):
            slot = src_ref[block, k]
            part = lax.dot_general(
                tiles_ref[i, k], grad, (((0,), (0,)), ((), ())),
                preferred_element_type=jnp.float32,
            )
            out_ref[slot] += part

    @pl.when(step == pl.num_programs(0) - 1)
    def _():
        own = own_ref.shape[0]
        lent = low_ref.shape[0]
        own_ref[...] = out_ref[:own]
        low_ref[...] = out_ref[own : own + lent].astype(low_ref.dtype)
        high_ref[...] = out_ref[own + lent :].astype(high_ref.dtype)


def block_slot_grad(slot_ids, tile_data, grad_blocks, pre_blocks, slot_count):
    blocks, listed, rows, _ = tile_data.shape
    width = grad_blocks.shape[-1]
    lent = (slot_count - blocks) // 2
    block_spec = pl.BlockSpec((GROUP, rows, width), lambda g, src: (g, 0, 0))
    whole = lambda count: pl.BlockSpec((count, rows, width), lambda g, src: (0, 0, 0))
    return pl.pallas_call(
        slot_grad_kernel,
        grid_spec=pltpu.PrefetchScalarGridSpec(
            num_scalar_prefetch=1,
            grid=(blocks // GROUP,),
            in_specs=[
                pl.BlockSpec((GROUP, listed, rows, rows), lambda g, src: (g, 0, 0, 0)),
                block_spec,
                block_spec,
            ],
            out_specs=[whole(blocks), whole(lent), whole(lent), block_spec],
            scratch_shapes=[pltpu.VMEM((slot_count, rows, width), jnp.float32)],
        ),
        out_shape=[
            jax.ShapeDtypeStruct((blocks, rows, width), jnp.float32),
            jax.ShapeDtypeStruct((lent, rows, width), jnp.bfloat16),
            jax.ShapeDtypeStruct((lent, rows, width), jnp.bfloat16),
            jax.ShapeDtypeStruct((blocks, rows, width), jnp.bfloat16),
        ],
        compiler_params=pltpu.CompilerParams(dimension_semantics=("arbitrary",)),
    )(slot_ids, tile_data, grad_blocks, pre_blocks)


def fold_kernel(lists_ref, slot_ref, lower_ref, upper_ref, out_ref, acc_ref):
    acc_ref[...] = slot_ref[...]
    for i in range(lower_ref.shape[0]):
        block = lists_ref[1, i]
        acc_ref[block] += lower_ref[i].astype(jnp.float32)
    for i in range(upper_ref.shape[0]):
        block = lists_ref[0, i]
        acc_ref[block] += upper_ref[i].astype(jnp.float32)
    out_ref[...] = acc_ref[...].astype(out_ref.dtype)


def fold_lent(own_lists, slot_grad, from_lower, from_upper, blocks):
    _, rows, width = slot_grad.shape
    lent = from_lower.shape[0]
    return pl.pallas_call(
        fold_kernel,
        grid_spec=pltpu.PrefetchScalarGridSpec(
            num_scalar_prefetch=1,
            grid=(1,),
            in_specs=[
                pl.BlockSpec((blocks, rows, width), lambda g, lists: (0, 0, 0)),
                pl.BlockSpec((lent, rows, width), lambda g, lists: (0, 0, 0)),
                pl.BlockSpec((lent, rows, width), lambda g, lists: (0, 0, 0)),
            ],
            out_specs=pl.BlockSpec((blocks, rows, width), lambda g, lists: (0, 0, 0)),
            scratch_shapes=[pltpu.VMEM((blocks, rows, width), jnp.float32)],
        ),
        out_shape=jax.ShapeDtypeStruct((blocks, rows, width), jnp.bfloat16),
    )(own_lists, slot_grad, from_lower, from_upper)


def to_upper(x, axis):
    count = lax.axis_size(axis)
    return lax.ppermute(x, axis, [(i, (i + 1) % count) for i in range(count)])


def to_lower(x, axis):
    count = lax.axis_size(axis)
    return lax.ppermute(x, axis, [((i + 1) % count, i) for i in range(count)])


def all_reduce(x, axes, scale):
    count = lax.axis_size(axes)
    width = x.shape[-1]
    pieces = x.reshape(count, -1, width).astype(jnp.bfloat16)
    received = lax.all_to_all(pieces, axes, 0, 0, tiled=True)
    mine = (received.astype(jnp.float32).sum(0) * scale).astype(jnp.bfloat16)
    spread = jnp.broadcast_to(mine[None], (count,) + mine.shape)
    gathered = lax.all_to_all(spread, axes, 0, 0, tiled=True)
    return gathered.astype(jnp.float32).reshape(x.shape)


def silu_grad(pre):
    sig = jax.nn.sigmoid(pre)
    return sig * (1.0 + pre * (1.0 - sig))


def per_device(hits, tiles, sources, send_list, w_message, w_self, cotangent):
    blocks_here = tiles.shape[1]
    tile_rows = tiles.shape[3]
    width = hits.shape[2]
    lent = send_list.shape[3]
    listed = tiles.shape[2]
    sector_here = lax.axis_index("sector")
    lists = send_list[0]
    own_lists = lax.dynamic_index_in_dim(lists, sector_here, 0, keepdims=False)
    tile_data = tiles[0]
    slot_ids = sources[0]
    slot_count = blocks_here + 2 * lent
    current = hits[0]
    saved = []
    for layer_index in range(LAYERS):
        message = jnp.dot(
            current, w_message[layer_index], preferred_element_type=jnp.float32
        ).astype(jnp.bfloat16)
        message_blocks = message.reshape(blocks_here, tile_rows, width)
        current_blocks = current.reshape(blocks_here, tile_rows, width)

        def lent_message(indices):
            return jnp.dot(
                current_blocks[indices].reshape(-1, width), w_message[layer_index],
                preferred_element_type=jnp.float32,
            ).astype(jnp.bfloat16).reshape(lent, tile_rows, width)

        from_lower = to_upper(lent_message(own_lists[0]), "sector")
        from_upper = to_lower(lent_message(own_lists[1]), "sector")
        pre, following = block_layer(
            slot_ids, tile_data, message_blocks, jnp.concatenate([from_lower, from_upper]),
            current.reshape(message_blocks.shape),
            w_self[layer_index],
        )
        saved.append((current, pre.reshape(-1, width)))
        current = following.reshape(-1, width)
    grad = cotangent[0]
    message_steps = [None] * LAYERS
    self_steps = [None] * LAYERS
    for layer_index in reversed(range(LAYERS)):
        layer_in, pre = saved[layer_index]
        own_grad, low_grad, high_grad, dpre_blocks = block_slot_grad(
            slot_ids, tile_data, grad.reshape(blocks_here, tile_rows, width),
            pre.reshape(blocks_here, tile_rows, width), slot_count,
        )
        dpre = dpre_blocks.reshape(-1, width)
        lent_down_grad = to_upper(high_grad, "sector")
        lent_up_grad = to_lower(low_grad, "sector")
        dmessage = fold_lent(
            own_lists, own_grad, lent_down_grad, lent_up_grad, blocks_here
        ).reshape(-1, width)
        self_part = jnp.dot(layer_in.T, dpre, preferred_element_type=jnp.float32)
        message_part = jnp.dot(layer_in.T, dmessage, preferred_element_type=jnp.float32)
        message_steps[layer_index] = message_part
        self_steps[layer_index] = self_part
        grad = grad + jnp.dot(dpre, w_self[layer_index].T, preferred_element_type=jnp.float32)
        grad = grad + jnp.dot(
            dmessage, w_message[layer_index].T, preferred_element_type=jnp.float32
        )
    message_total = jnp.stack(message_steps)
    self_total = jnp.stack(self_steps)
    total_rows = blocks_here * tile_rows * lax.axis_size(("dp", "sector"))
    scale = 1.0 / jnp.sqrt(jnp.float32(total_rows))
    both = all_reduce(jnp.stack([message_total, self_total]), ("dp", "sector"), scale)
    return (current[None], grad[None], both[0], both[1])


def solution(mesh):
    in_specs = (
        P("dp", "sector", None),
        P("dp", "sector", None, None, None),
        P("dp", "sector", None),
        P("dp", None, None, None),
        P(),
        P(),
        P("dp", "sector", None),
    )
    out_specs = (P("dp", "sector", None), P("dp", "sector", None), P(), P())
    return jax.shard_map(
        per_device, mesh=mesh, in_specs=in_specs, out_specs=out_specs, check_vma=False
    )
```

```python
import jax
import jax.numpy as jnp
from jax import lax
from jax.experimental import pallas as pl
from jax.experimental.pallas import tpu as pltpu
from jax.sharding import PartitionSpec as P

LAYERS = 2
GROUP = 8


def slot_rows(own_ref, lower_ref, upper_ref, slot):
    own = own_ref.shape[0]
    lent = lower_ref.shape[0]
    return jnp.where(
        slot < own,
        own_ref[jnp.minimum(slot, own - 1)],
        jnp.where(
            slot < own + lent,
            lower_ref[jnp.clip(slot - own, 0, lent - 1)],
            upper_ref[jnp.clip(slot - own - lent, 0, lent - 1)],
        ),
    )


def layer_kernel(src_ref, tiles_ref, own_ref, lower_ref, upper_ref, hits_ref, weight_ref, pre_ref, out_ref):
    step = pl.program_id(0)
    listed = tiles_ref.shape[1]
    for i in range(GROUP):
        block = step * GROUP + i
        lhs = jnp.concatenate([tiles_ref[i, k] for k in range(listed)], axis=1)
        rhs = jnp.concatenate(
            [slot_rows(own_ref, lower_ref, upper_ref, src_ref[block, k]) for k in range(listed)], axis=0
        )
        rows = hits_ref[i]
        pre = jnp.dot(lhs, rhs, preferred_element_type=jnp.float32) + jnp.dot(
            rows, weight_ref[...], preferred_element_type=jnp.float32
        )
        pre_ref[i] = pre
        out_ref[i] = (rows.astype(jnp.float32) + pre * jax.nn.sigmoid(pre)).astype(
            out_ref.dtype
        )


def block_layer(slot_ids, tile_data, own_table, lower_table, upper_table, hit_blocks, weight):
    blocks, listed, rows, _ = tile_data.shape
    width = own_table.shape[-1]
    block_spec = pl.BlockSpec((GROUP, rows, width), lambda g, src: (g, 0, 0))
    return pl.pallas_call(
        layer_kernel,
        grid_spec=pltpu.PrefetchScalarGridSpec(
            num_scalar_prefetch=1,
            grid=(blocks // GROUP,),
            in_specs=[
                pl.BlockSpec((GROUP, listed, rows, rows), lambda g, src: (g, 0, 0, 0)),
                pl.BlockSpec(own_table.shape, lambda g, src: (0, 0, 0)),
                pl.BlockSpec(lower_table.shape, lambda g, src: (0, 0, 0)),
                pl.BlockSpec(upper_table.shape, lambda g, src: (0, 0, 0)),
                block_spec,
                pl.BlockSpec(weight.shape, lambda g, src: (0, 0)),
            ],
            out_specs=[block_spec, block_spec],
        ),
        out_shape=[
            jax.ShapeDtypeStruct((blocks, rows, width), jnp.float32),
            jax.ShapeDtypeStruct((blocks, rows, width), hit_blocks.dtype),
        ],
    )(slot_ids, tile_data, own_table, lower_table, upper_table, hit_blocks, weight)


def slot_grad_kernel(src_ref, tiles_ref, grad_ref, pre_ref, own_ref, low_ref, high_ref, dpre_ref, out_ref):
    step = pl.program_id(0)

    @pl.when(step == 0)
    def _():
        out_ref[...] = jnp.zeros(out_ref.shape, out_ref.dtype)

    for i in range(GROUP):
        block = step * GROUP + i
        pre = pre_ref[i]
        sig = jax.nn.sigmoid(pre)
        grad = (grad_ref[i] * (sig * (1.0 + pre * (1.0 - sig)))).astype(dpre_ref.dtype)
        dpre_ref[i] = grad
        for k in range(tiles_ref.shape[1]):
            slot = src_ref[block, k]
            part = lax.dot_general(
                tiles_ref[i, k], grad, (((0,), (0,)), ((), ())),
                preferred_element_type=jnp.float32,
            )
            out_ref[slot] += part

    @pl.when(step == pl.num_programs(0) - 1)
    def _():
        own = own_ref.shape[0]
        lent = low_ref.shape[0]
        own_ref[...] = out_ref[:own]
        low_ref[...] = out_ref[own : own + lent].astype(low_ref.dtype)
        high_ref[...] = out_ref[own + lent :].astype(high_ref.dtype)


def block_slot_grad(slot_ids, tile_data, grad_blocks, pre_blocks, slot_count):
    blocks, listed, rows, _ = tile_data.shape
    width = grad_blocks.shape[-1]
    lent = (slot_count - blocks) // 2
    block_spec = pl.BlockSpec((GROUP, rows, width), lambda g, src: (g, 0, 0))
    whole = lambda count: pl.BlockSpec((count, rows, width), lambda g, src: (0, 0, 0))
    return pl.pallas_call(
        slot_grad_kernel,
        grid_spec=pltpu.PrefetchScalarGridSpec(
            num_scalar_prefetch=1,
            grid=(blocks // GROUP,),
            in_specs=[
                pl.BlockSpec((GROUP, listed, rows, rows), lambda g, src: (g, 0, 0, 0)),
                block_spec,
                block_spec,
            ],
            out_specs=[whole(blocks), whole(lent), whole(lent), block_spec],
            scratch_shapes=[pltpu.VMEM((slot_count, rows, width), jnp.float32)],
        ),
        out_shape=[
            jax.ShapeDtypeStruct((blocks, rows, width), jnp.float32),
            jax.ShapeDtypeStruct((lent, rows, width), jnp.bfloat16),
            jax.ShapeDtypeStruct((lent, rows, width), jnp.bfloat16),
            jax.ShapeDtypeStruct((blocks, rows, width), jnp.bfloat16),
        ],
        compiler_params=pltpu.CompilerParams(dimension_semantics=("arbitrary",)),
    )(slot_ids, tile_data, grad_blocks, pre_blocks)


def fold_kernel(lists_ref, slot_ref, lower_ref, upper_ref, out_ref, acc_ref):
    acc_ref[...] = slot_ref[...]
    for i in range(lower_ref.shape[0]):
        block = lists_ref[1, i]
        acc_ref[block] += lower_ref[i].astype(jnp.float32)
    for i in range(upper_ref.shape[0]):
        block = lists_ref[0, i]
        acc_ref[block] += upper_ref[i].astype(jnp.float32)
    out_ref[...] = acc_ref[...].astype(out_ref.dtype)


def fold_lent(own_lists, slot_grad, from_lower, from_upper, blocks):
    _, rows, width = slot_grad.shape
    lent = from_lower.shape[0]
    return pl.pallas_call(
        fold_kernel,
        grid_spec=pltpu.PrefetchScalarGridSpec(
            num_scalar_prefetch=1,
            grid=(1,),
            in_specs=[
                pl.BlockSpec((blocks, rows, width), lambda g, lists: (0, 0, 0)),
                pl.BlockSpec((lent, rows, width), lambda g, lists: (0, 0, 0)),
                pl.BlockSpec((lent, rows, width), lambda g, lists: (0, 0, 0)),
            ],
            out_specs=pl.BlockSpec((blocks, rows, width), lambda g, lists: (0, 0, 0)),
            scratch_shapes=[pltpu.VMEM((blocks, rows, width), jnp.float32)],
        ),
        out_shape=jax.ShapeDtypeStruct((blocks, rows, width), jnp.bfloat16),
    )(own_lists, slot_grad, from_lower, from_upper)


def to_upper(x, axis):
    count = lax.axis_size(axis)
    return lax.ppermute(x, axis, [(i, (i + 1) % count) for i in range(count)])


def to_lower(x, axis):
    count = lax.axis_size(axis)
    return lax.ppermute(x, axis, [((i + 1) % count, i) for i in range(count)])


def all_reduce(x, axes, scale):
    count = lax.axis_size(axes)
    width = x.shape[-1]
    pieces = x.reshape(count, -1, width).astype(jnp.bfloat16)
    received = lax.all_to_all(pieces, axes, 0, 0, tiled=True)
    mine = (received.astype(jnp.float32).sum(0) * scale).astype(jnp.bfloat16)
    spread = jnp.broadcast_to(mine[None], (count,) + mine.shape)
    gathered = lax.all_to_all(spread, axes, 0, 0, tiled=True)
    return gathered.astype(jnp.float32).reshape(x.shape)


def silu_grad(pre):
    sig = jax.nn.sigmoid(pre)
    return sig * (1.0 + pre * (1.0 - sig))


def per_device(hits, tiles, sources, send_list, w_message, w_self, cotangent):
    blocks_here = tiles.shape[1]
    tile_rows = tiles.shape[3]
    width = hits.shape[2]
    lent = send_list.shape[3]
    listed = tiles.shape[2]
    sector_here = lax.axis_index("sector")
    lists = send_list[0]
    own_lists = lax.dynamic_index_in_dim(lists, sector_here, 0, keepdims=False)
    tile_data = tiles[0]
    slot_ids = sources[0]
    slot_count = blocks_here + 2 * lent
    current = hits[0]
    saved = []
    for layer_index in range(LAYERS):
        message = jnp.dot(
            current, w_message[layer_index], preferred_element_type=jnp.float32
        ).astype(jnp.bfloat16)
        message_blocks = message.reshape(blocks_here, tile_rows, width)
        from_lower = to_upper(message_blocks[own_lists[0]], "sector")
        from_upper = to_lower(message_blocks[own_lists[1]], "sector")
        pre, following = block_layer(
            slot_ids, tile_data, message_blocks, from_lower, from_upper,
            current.reshape(message_blocks.shape),
            w_self[layer_index],
        )
        saved.append((current, pre.reshape(-1, width)))
        current = following.reshape(-1, width)
    grad = cotangent[0]
    message_steps = [None] * LAYERS
    self_steps = [None] * LAYERS
    for layer_index in reversed(range(LAYERS)):
        layer_in, pre = saved[layer_index]
        own_grad, low_grad, high_grad, dpre_blocks = block_slot_grad(
            slot_ids, tile_data, grad.reshape(blocks_here, tile_rows, width),
            pre.reshape(blocks_here, tile_rows, width), slot_count,
        )
        dpre = dpre_blocks.reshape(-1, width)
        lent_down_grad = to_upper(high_grad, "sector")
        lent_up_grad = to_lower(low_grad, "sector")
        dmessage = fold_lent(
            own_lists, own_grad, lent_down_grad, lent_up_grad, blocks_here
        ).reshape(-1, width)
        self_part = jnp.dot(layer_in.T, dpre, preferred_element_type=jnp.float32)
        message_part = jnp.dot(layer_in.T, dmessage, preferred_element_type=jnp.float32)
        message_steps[layer_index] = message_part
        self_steps[layer_index] = self_part
        grad = grad + jnp.dot(dpre, w_self[layer_index].T, preferred_element_type=jnp.float32)
        grad = grad + jnp.dot(
            dmessage, w_message[layer_index].T, preferred_element_type=jnp.float32
        )
    message_total = jnp.stack(message_steps)
    self_total = jnp.stack(self_steps)
    total_rows = blocks_here * tile_rows * lax.axis_size(("dp", "sector"))
    scale = 1.0 / jnp.sqrt(jnp.float32(total_rows))
    both = all_reduce(jnp.stack([message_total, self_total]), ("dp", "sector"), scale)
    return (current[None], grad[None], both[0], both[1])


def solution(mesh):
    in_specs = (
        P("dp", "sector", None),
        P("dp", "sector", None, None, None),
        P("dp", "sector", None),
        P("dp", None, None, None),
        P(),
        P(),
        P("dp", "sector", None),
    )
    out_specs = (P("dp", "sector", None), P("dp", "sector", None), P(), P())
    return jax.shard_map(
        per_device, mesh=mesh, in_specs=in_specs, out_specs=out_specs, check_vma=False
    )
```
